128 devices in a mesh: wide: 16 (over x, y_hi, core), head: 8 (over z, y_lo).
Axes of the slice: x: 4, y: 4 (y_hi: 2, y_lo: 2; y = y_hi * 2 + y_lo), z: 4, core: 2. Of those that a mesh axis runs over, the one named last changes fastest.
Arguments:
- tokens: bfloat16 [16384, 2048], P('wide', 'head'), may hold values from -6 to 6
- lengths: int32 [32], P('wide'), may hold values from 32 to 512, as said below
- positions: int32 [32, 512], P('wide'), may hold values from 0 to 1022, as said below
- attn_gain: float32 [2048], replicated, may hold values from 0.1 to 1.9
- qkv_weight: float32 [2048, 6144], P('wide', 'head'), may hold values from -8 to 8
- lambdas: float32 [4, 8, 128], P(None, 'head'), may hold values from -0.6 to 0.6
- sub_gain: float32 [8, 256], P('head'), may hold values from 0.1 to 1.9
- out_weight: float32 [2048, 2048], P('head', 'wide'), may hold values from -0.125 to 0.125
- ffn_gain: float32 [2048], replicated, may hold values from 0.1 to 1.9
- gate_up_weight: float32 [2048, 2, 5632], P('wide', None, 'head'), may hold values from -0.125 to 0.125
- down_weight: float32 [5632, 2048], P('head', 'wide'), may hold values from -0.078125 to 0.078125
Outputs:
- result: bfloat16 [16384, 2048], P('wide', 'head')
The draws below stay inside these ranges and needn't reach their ends.
Inputs may be any that keep to these rules, and one draw needn't show every extreme that they name: `lengths`: each prompt's live slots are its first ones; some prompt has all 512 slots live. Each prompt's positions start at 0 and rise by 1 or 2 from slot to slot; some prompt's positions rise by 2 throughout.
All inputs are finite; a program needn't handle non-finite values.
Results may differ from the reference program's by a relative error of at most 0.017.
The reference program's roundings to bfloat16 on the way count: a program that leaves them out, or rounds other values in their place, can miss the bound.
Values may be sent and summed in bfloat16 or wider, within the bound.
No kernel may reach another device: no remote copies, remote signals or barrier semaphores. Data moves between devices by JAX's collectives and lax.ppermute only.
A program may use at most 128 MiB of HBM per device.

```python
import jax
import jax.numpy as jnp
from jax import lax

D = 2048
HEADS = 8
HALF = 128
VDIM = 256
FF = 5632
SLOTS = 512
PROMPTS = 32
N_HEAD = 8


def draw_lengths(key, part):
    first = jax.random.fold_in(key, 11)
    second = jax.random.fold_in(key, 12)
    base = jax.random.randint(first, (PROMPTS,), SLOTS // 16, SLOTS + 1)
    chosen = jax.random.randint(second, (), 0, PROMPTS)
    return jnp.where(jnp.arange(PROMPTS) == chosen, SLOTS, base).astype(jnp.int32)


def draw_positions(key, part):
    steps = jax.random.randint(jax.random.fold_in(key, 21), (PROMPTS, SLOTS), 1, 3)
    chosen = jax.random.randint(jax.random.fold_in(key, 22), (), 0, PROMPTS)
    steps = jnp.where((jnp.arange(PROMPTS) == chosen)[:, None], 2, steps)
    return (jnp.cumsum(steps, axis=1) - steps[:, :1]).astype(jnp.int32)


def draw_qkv_weight(key, part):
    width = 4 * HALF + VDIM
    base = jax.random.truncated_normal(jax.random.fold_in(key, 31), -6.0, 6.0, (D, HEADS * width), jnp.float32)
    base = base * D ** (-0.5)
    return base.astype(jnp.float32)


def steps_of(key, extent, shards, low, largest):
    def one(dim, blocks):
        heights = jax.random.uniform(jax.random.fold_in(jax.random.fold_in(key, 6), dim), (blocks,), jnp.float32, low / len(shards), largest / len(shards))
        return jnp.repeat(jnp.exp(heights), extent[dim] // blocks).reshape((-1,) + (1,) * (len(extent) - dim - 1))

    factor_of = one(*shards[0])
    for cut in shards[1:]:
        factor_of = factor_of * one(*cut)
    return factor_of


def centred(stream_key, shape, spread, reach, shards=(), held_as=jnp.bfloat16):
    entries = jax.random.normal(stream_key, shape, jnp.float32) * spread
    if len(shards) > 0:
        entries = steps_of(stream_key, shape, shards, -0.22, 0.18) * entries
    return jnp.clip(entries, min=-reach, max=reach).astype(held_as)


def setup_inputs(seed: int = 0) -> dict:
    key_of = jax.random.split(jax.random.key(seed), 12)
    tokens = centred(key_of[0], (PROMPTS * SLOTS, D), 1.0, 6.0, ((0, 16), (1, 8)))
    lengths = draw_lengths(jax.random.fold_in(key_of[11], 71), 0)
    positions = draw_positions(jax.random.fold_in(key_of[11], 71), 0)
    attn_gain = jnp.clip(1.0 + 0.18 * jax.random.normal(key_of[3], (D,), jnp.float32), 0.1, 1.9)
    qkv_weight = draw_qkv_weight(jax.random.fold_in(key_of[11], 71), 0)
    lambdas = centred(key_of[5], (4, HEADS, HALF), 0.15, 0.6, ((1, 8),), jnp.float32)
    sub_gain = jnp.clip(1.0 + 0.18 * jax.random.normal(key_of[6], (HEADS, VDIM), jnp.float32), 0.1, 1.9)
    out_weight = centred(key_of[7], (HEADS * VDIM, D), (HEADS * VDIM) ** -0.5, 0.125, ((0, 8), (1, 16)), jnp.float32)
    ffn_gain = jnp.clip(1.0 + 0.18 * jax.random.normal(key_of[8], (D,), jnp.float32), 0.1, 1.9)
    gate_up_weight = centred(key_of[9], (D, 2, FF), D ** -0.5, 0.125, ((0, 16), (2, 8)), jnp.float32)
    down_weight = centred(key_of[10], (FF, D), FF ** -0.5, 0.078125, ((0, 8), (1, 16)), jnp.float32)
    return {"tokens": tokens, "lengths": lengths, "positions": positions, "attn_gain": attn_gain, "qkv_weight": qkv_weight, "lambdas": lambdas, "sub_gain": sub_gain, "out_weight": out_weight, "ffn_gain": ffn_gain, "gate_up_weight": gate_up_weight, "down_weight": down_weight}


lambda_base = 0.2

def rms_scale(values, gain):
    flat = values.astype(jnp.float32)
    return flat * lax.rsqrt(lax.optimization_barrier(jnp.mean(flat * flat, axis=-1, keepdims=True)) + 1e-05) * gain

def rotate(quads, places):
    width = quads.shape[-1]
    half = width // 2
    freq = 10000.0 ** (-(jnp.arange(half, dtype=jnp.float32) * 2.0 / width))
    angle = places.astype(jnp.float32)[:, None] * freq[None, :]
    cosine = jnp.cos(angle)[:, None, None, :]
    sine = jnp.sin(angle)[:, None, None, :]
    first = quads[..., :half]
    second = quads[..., half:]
    return jnp.concatenate([first * cosine - second * sine, second * cosine + first * sine], axis=-1)

def diff_attend(first_q, second_q, first_k, second_k, values, rows_at, length, balance, gain):
    scale = first_q.shape[-1] ** (-0.5)
    keys_at = jnp.arange(first_k.shape[0], dtype=jnp.int32)
    allowed = (keys_at[None, :] <= rows_at[:, None]) & (keys_at[None, :] < length)
    one = jnp.einsum('rhd,shd->hrs', first_q.astype(jnp.float32), first_k.astype(jnp.float32)) * scale
    two = jnp.einsum('rhd,shd->hrs', second_q.astype(jnp.float32), second_k.astype(jnp.float32)) * scale
    one = jax.nn.softmax(jnp.where(allowed[None], one, -1e+30), axis=-1)
    two = jax.nn.softmax(jnp.where(allowed[None], two, -1e+30), axis=-1)
    weights = (one - balance[:, None, None] * two).astype(jnp.bfloat16)
    merged = jnp.einsum('hrs,shv->rhv', weights.astype(jnp.float32), values.astype(jnp.float32))
    merged = rms_scale(merged, gain[None]) * (1.0 - lambda_base)
    merged = jnp.where((rows_at < length)[:, None, None], merged, 0.0)
    return merged.reshape(merged.shape[0], -1).astype(jnp.bfloat16)

def group_sum(left, right, groups):
    rows = left.shape[0]
    inner = left.shape[1] // groups
    lhs = left.reshape(rows, groups, inner).astype(jnp.float32)
    rhs = right.reshape(groups, inner, right.shape[1]).astype(jnp.float32)
    parts = jnp.einsum('sgk,gkd->gsd', lhs, rhs)
    rounded = lax.optimization_barrier(parts.astype(jnp.bfloat16))
    return lax.optimization_barrier(jnp.sum(rounded.astype(jnp.float32), axis=0))

def reference(tokens, lengths, positions, attn_gain, qkv_weight, lambdas, sub_gain, out_weight, ffn_gain, gate_up_weight, down_weight):
    qkv_b = qkv_weight.astype(jnp.bfloat16)
    out_b = out_weight.astype(jnp.bfloat16)
    gate_up_b = gate_up_weight.astype(jnp.bfloat16).reshape(D, 2 * FF)
    down_b = down_weight.astype(jnp.bfloat16)
    balance = jnp.exp(lax.optimization_barrier(jnp.sum(lambdas[0] * lambdas[1], -1))) - jnp.exp(lax.optimization_barrier(jnp.sum(lambdas[2] * lambdas[3], -1))) + lambda_base
    width = 4 * HALF + VDIM

    def layer_one(inputs):
        stream, length, places = inputs
        normed = rms_scale(stream, attn_gain).astype(jnp.bfloat16)
        joined = jnp.dot(normed, qkv_b, preferred_element_type=jnp.float32).reshape(SLOTS, HEADS, width)
        quads = rotate(joined[..., :4 * HALF].reshape(SLOTS, HEADS, 4, HALF), places).astype(jnp.bfloat16)
        values = joined[..., 4 * HALF:].astype(jnp.bfloat16)
        attn = diff_attend(quads[:, :, 0], quads[:, :, 1], quads[:, :, 2], quads[:, :, 3], values, jnp.arange(SLOTS, dtype=jnp.int32), length, balance, sub_gain)
        mix = group_sum(attn, out_b, N_HEAD)
        middle = (stream.astype(jnp.float32) + mix).astype(jnp.bfloat16)
        normed2 = rms_scale(middle, ffn_gain).astype(jnp.bfloat16)
        both = jnp.dot(normed2, gate_up_b, preferred_element_type=jnp.float32)
        hidden = (jax.nn.silu(both[:, :FF]) * both[:, FF:]).astype(jnp.bfloat16)
        ffn = group_sum(hidden, down_b, N_HEAD)
        return (middle.astype(jnp.float32) + ffn).astype(jnp.bfloat16)
    outputs = lax.map(layer_one, (tokens.reshape(PROMPTS, SLOTS, D), lengths, positions))
    return outputs.reshape(PROMPTS * SLOTS, D)
```

```python
import jax
import jax.numpy as jnp
from jax import lax
from jax.sharding import PartitionSpec as P

HALF = 128
VDIM = 256


lambda_base = 0.2


def rms_scale(values, gain):
    flat = values.astype(jnp.float32)
    return flat * lax.rsqrt(jnp.mean(flat * flat, axis=-1, keepdims=True) + 1e-05) * gain


def rotate(quads, places):
    width = quads.shape[-1]
    half = width // 2
    freq = 10000.0 ** (-(jnp.arange(half, dtype=jnp.float32) * 2.0 / width))
    angle = places.astype(jnp.float32)[:, None] * freq[None, :]
    cosine = jnp.cos(angle)[:, None, None, :]
    sine = jnp.sin(angle)[:, None, None, :]
    first = quads[..., :half]
    second = quads[..., half:]
    return jnp.concatenate(
        [first * cosine - second * sine, second * cosine + first * sine], axis=-1
    )


def gather_blocks(x, axis, n, dim):
    spread = jnp.broadcast_to(x[None], (n,) + x.shape)
    got = lax.all_to_all(spread, axis, 0, 0, tiled=True)
    got = jnp.moveaxis(got, 0, dim)
    shape = list(x.shape)
    shape[dim] *= n
    return got.reshape(shape)


def scatter_sum(terms, axis, n):
    rows, cols = terms.shape
    parts = terms.astype(jnp.bfloat16).reshape(rows, n, cols // n)
    got = lax.all_to_all(parts, axis, 1, 1, tiled=True)
    return jnp.sum(got.astype(jnp.float32), axis=1)


def diff_attend(first_q, second_q, first_k, second_k, values, rows_at, length, balance, gain):
    scale = first_q.shape[-1] ** (-0.5)
    keys_at = jnp.arange(first_k.shape[0], dtype=jnp.int32)
    allowed = (keys_at[None, :] <= rows_at[:, None]) & (keys_at[None, :] < length)
    one = jnp.einsum("rhd,shd->hrs", first_q, first_k, preferred_element_type=jnp.float32) * scale
    two = jnp.einsum("rhd,shd->hrs", second_q, second_k, preferred_element_type=jnp.float32) * scale
    one = jax.nn.softmax(jnp.where(allowed[None], one, -1e30), axis=-1)
    two = jax.nn.softmax(jnp.where(allowed[None], two, -1e30), axis=-1)
    weights = (one - balance[:, None, None] * two).astype(jnp.bfloat16)
    merged = jnp.einsum("hrs,shv->rhv", weights, values, preferred_element_type=jnp.float32)
    merged = rms_scale(merged, gain[None]) * (1.0 - lambda_base)
    merged = jnp.where((rows_at < length)[:, None, None], merged, 0.0)
    return merged.reshape(merged.shape[0], -1).astype(jnp.bfloat16)


def body(
    tokens,
    lengths,
    positions,
    attn_gain,
    qkv_weight,
    lambdas,
    sub_gain,
    out_weight,
    ffn_gain,
    gate_up_weight,
    down_weight,
):
    prompts_here = lengths.shape[0]
    slots = positions.shape[1]
    width = 4 * HALF + VDIM
    n_head = lax.axis_size("head")
    n_wide = lax.axis_size("wide")
    full_rows = gather_blocks(tokens, "head", n_head, 1)
    normed = rms_scale(full_rows, attn_gain).astype(jnp.bfloat16)
    qkv_local = qkv_weight.astype(jnp.bfloat16)
    columns = normed
    joined = jnp.dot(
        columns,
        gather_blocks(qkv_local, "wide", n_wide, 0),
        preferred_element_type=jnp.float32,
    )
    heads_here = qkv_local.shape[1] // width
    balance = (
        jnp.exp(jnp.sum(lambdas[0] * lambdas[1], -1))
        - jnp.exp(jnp.sum(lambdas[2] * lambdas[3], -1))
        + lambda_base
    )
    outputs = []
    for prompt in range(prompts_here):
        block = joined[prompt * slots : (prompt + 1) * slots].reshape(slots, heads_here, width)
        quads = rotate(
            block[..., : 4 * HALF].reshape(slots, heads_here, 4, HALF), positions[prompt]
        ).astype(jnp.bfloat16)
        values = block[..., 4 * HALF :].astype(jnp.bfloat16)
        length = lengths[prompt]
        first_k = quads[:, :, 2]
        second_k = quads[:, :, 3]
        attended = diff_attend(
            quads[:, :, 0],
            quads[:, :, 1],
            first_k,
            second_k,
            values,
            jnp.arange(slots, dtype=jnp.int32),
            length,
            balance,
            sub_gain,
        )
        outputs.append(attended)
    attn = jnp.concatenate(outputs, axis=0)
    mix_terms = jnp.dot(
        attn,
        gather_blocks(out_weight.astype(jnp.bfloat16), "wide", n_wide, 1),
        preferred_element_type=jnp.float32,
    )
    mix = scatter_sum(mix_terms, "head", n_head)
    middle = (tokens.astype(jnp.float32) + mix).astype(jnp.bfloat16)
    middle_full = gather_blocks(middle, "head", n_head, 1)
    normed2 = rms_scale(middle_full, ffn_gain).astype(jnp.bfloat16)
    gate_up_local = gate_up_weight.astype(jnp.bfloat16)
    columns = normed2
    both = jnp.einsum(
        "td,dgf->tgf",
        columns,
        gather_blocks(gate_up_local, "wide", n_wide, 0),
        preferred_element_type=jnp.float32,
    )
    hidden = (jax.nn.silu(both[:, 0]) * both[:, 1]).astype(jnp.bfloat16)
    ffn_terms = jnp.dot(
        hidden,
        gather_blocks(down_weight.astype(jnp.bfloat16), "wide", n_wide, 1),
        preferred_element_type=jnp.float32,
    )
    ffn = scatter_sum(ffn_terms, "head", n_head)
    return (middle.astype(jnp.float32) + ffn).astype(jnp.bfloat16)


def solution(mesh):
    placed = (
        P("wide", "head"),
        P("wide"),
        P("wide", None),
        P(),
        P("wide", "head"),
        P(None, "head", None),
        P("head", None),
        P("head", "wide"),
        P(),
        P("wide", None, "head"),
        P("head", "wide"),
    )
    return jax.shard_map(
        body, mesh=mesh, in_specs=placed, out_specs=P("wide", "head"), check_vma=False
    )
```

```python
import jax
import jax.numpy as jnp
from jax import lax
from jax.sharding import PartitionSpec as P

HALF = 128
VDIM = 256


lambda_base = 0.2


def rms_scale(values, gain):
    flat = values.astype(jnp.float32)
    return flat * lax.rsqrt(jnp.mean(flat * flat, axis=-1, keepdims=True) + 1e-05) * gain


def rotate(quads, places):
    width = quads.shape[-1]
    half = width // 2
    freq = 10000.0 ** (-(jnp.arange(half, dtype=jnp.float32) * 2.0 / width))
    angle = places.astype(jnp.float32)[:, None] * freq[None, :]
    cosine = jnp.cos(angle)[:, None, None, :]
    sine = jnp.sin(angle)[:, None, None, :]
    first = quads[..., :half]
    second = quads[..., half:]
    return jnp.concatenate(
        [first * cosine - second * sine, second * cosine + first * sine], axis=-1
    )


def gather_blocks(x, axis, n, dim):
    spread = jnp.broadcast_to(x[None], (n,) + x.shape)
    got = lax.all_to_all(spread, axis, 0, 0, tiled=True)
    got = jnp.moveaxis(got, 0, dim)
    shape = list(x.shape)
    shape[dim] *= n
    return got.reshape(shape)


def scatter_sum(terms, axis, n):
    rows, cols = terms.shape
    parts = terms.astype(jnp.bfloat16).reshape(rows, n, cols // n)
    got = lax.all_to_all(parts, axis, 1, 1, tiled=True)
    return jnp.sum(got.astype(jnp.float32), axis=1)


def diff_attend(first_q, second_q, first_k, second_k, values, rows_at, length, balance, gain):
    scale = first_q.shape[-1] ** (-0.5)
    keys_at = jnp.arange(first_k.shape[0], dtype=jnp.int32)
    allowed = (keys_at[None, :] <= rows_at[:, None]) & (keys_at[None, :] < length)
    one = jnp.einsum("rhd,shd->hrs", first_q, first_k, preferred_element_type=jnp.float32) * scale
    two = jnp.einsum("rhd,shd->hrs", second_q, second_k, preferred_element_type=jnp.float32) * scale
    one = jax.nn.softmax(jnp.where(allowed[None], one, -1e30), axis=-1)
    two = jax.nn.softmax(jnp.where(allowed[None], two, -1e30), axis=-1)
    weights = (one - balance[:, None, None] * two).astype(jnp.bfloat16)
    merged = jnp.einsum("hrs,shv->rhv", weights, values, preferred_element_type=jnp.float32)
    merged = rms_scale(merged, gain[None]) * (1.0 - lambda_base)
    merged = jnp.where((rows_at < length)[:, None, None], merged, 0.0)
    return merged.reshape(merged.shape[0], -1).astype(jnp.bfloat16)


def body(
    tokens,
    lengths,
    positions,
    attn_gain,
    qkv_weight,
    lambdas,
    sub_gain,
    out_weight,
    ffn_gain,
    gate_up_weight,
    down_weight,
):
    prompts_here = lengths.shape[0]
    slots = positions.shape[1]
    width = 4 * HALF + VDIM
    n_head = lax.axis_size("head")
    n_wide = lax.axis_size("wide")
    full_rows = gather_blocks(tokens, "head", n_head, 1)
    normed = rms_scale(full_rows, attn_gain).astype(jnp.bfloat16)
    qkv_local = qkv_weight.astype(jnp.bfloat16)
    columns = normed
    joined = jnp.dot(
        columns,
        lax.all_gather(qkv_local, "wide", axis=0, tiled=True),
        preferred_element_type=jnp.float32,
    )
    heads_here = qkv_local.shape[1] // width
    balance = (
        jnp.exp(jnp.sum(lambdas[0] * lambdas[1], -1))
        - jnp.exp(jnp.sum(lambdas[2] * lambdas[3], -1))
        + lambda_base
    )
    outputs = []
    for prompt in range(prompts_here):
        block = joined[prompt * slots : (prompt + 1) * slots].reshape(slots, heads_here, width)
        quads = rotate(
            block[..., : 4 * HALF].reshape(slots, heads_here, 4, HALF), positions[prompt]
        ).astype(jnp.bfloat16)
        values = block[..., 4 * HALF :].astype(jnp.bfloat16)
        length = lengths[prompt]
        first_k = quads[:, :, 2]
        second_k = quads[:, :, 3]
        attended = diff_attend(
            quads[:, :, 0],
            quads[:, :, 1],
            first_k,
            second_k,
            values,
            jnp.arange(slots, dtype=jnp.int32),
            length,
            balance,
            sub_gain,
        )
        outputs.append(attended)
    attn = jnp.concatenate(outputs, axis=0)
    mix_terms = jnp.dot(
        attn,
        lax.all_gather(out_weight.astype(jnp.bfloat16), "wide", axis=1, tiled=True),
        preferred_element_type=jnp.float32,
    )
    mix = scatter_sum(mix_terms, "head", n_head)
    middle = (tokens.astype(jnp.float32) + mix).astype(jnp.bfloat16)
    middle_full = gather_blocks(middle, "head", n_head, 1)
    normed2 = rms_scale(middle_full, ffn_gain).astype(jnp.bfloat16)
    gate_up_local = gate_up_weight.astype(jnp.bfloat16)
    columns = normed2
    both = jnp.einsum(
        "td,dgf->tgf",
        columns,
        lax.all_gather(gate_up_local, "wide", axis=0, tiled=True),
        preferred_element_type=jnp.float32,
    )
    hidden = (jax.nn.silu(both[:, 0]) * both[:, 1]).astype(jnp.bfloat16)
    ffn_terms = jnp.dot(
        hidden,
        lax.all_gather(down_weight.astype(jnp.bfloat16), "wide", axis=1, tiled=True),
        preferred_element_type=jnp.float32,
    )
    ffn = scatter_sum(ffn_terms, "head", n_head)
    return (middle.astype(jnp.float32) + ffn).astype(jnp.bfloat16)


def solution(mesh):
    placed = (
        P("wide", "head"),
        P("wide"),
        P("wide", None),
        P(),
        P("wide", "head"),
        P(None, "head", None),
        P("head", None),
        P("head", "wide"),
        P(),
        P("wide", None, "head"),
        P("head", "wide"),
    )
    return jax.shard_map(
        body, mesh=mesh, in_specs=placed, out_specs=P("wide", "head"), check_vma=False
    )
```

```python
import jax
import jax.numpy as jnp
from jax import lax
from jax.sharding import PartitionSpec as P

HALF = 128
VDIM = 256


lambda_base = 0.2


def rms_scale(values, gain):
    flat = values.astype(jnp.float32)
    return flat * lax.rsqrt(jnp.mean(flat * flat, axis=-1, keepdims=True) + 1e-05) * gain


def rotate(quads, places):
    width = quads.shape[-1]
    half = width // 2
    freq = 10000.0 ** (-(jnp.arange(half, dtype=jnp.float32) * 2.0 / width))
    angle = places.astype(jnp.float32)[:, None] * freq[None, :]
    cosine = jnp.cos(angle)[:, None, None, :]
    sine = jnp.sin(angle)[:, None, None, :]
    first = quads[..., :half]
    second = quads[..., half:]
    return jnp.concatenate(
        [first * cosine - second * sine, second * cosine + first * sine], axis=-1
    )


def gather_blocks(x, axis, n, dim):
    spread = jnp.broadcast_to(x[None], (n,) + x.shape)
    got = lax.all_to_all(spread, axis, 0, 0, tiled=True)
    got = jnp.moveaxis(got, 0, dim)
    shape = list(x.shape)
    shape[dim] *= n
    return got.reshape(shape)


def scatter_sum(terms, axis, n):
    rows, cols = terms.shape
    parts = terms.astype(jnp.bfloat16).reshape(rows, n, cols // n)
    got = lax.all_to_all(parts, axis, 1, 1, tiled=True)
    return jnp.sum(got.astype(jnp.float32), axis=1)


def diff_attend(first_q, second_q, first_k, second_k, values, rows_at, length, balance, gain):
    scale = first_q.shape[-1] ** (-0.5)
    keys_at = jnp.arange(first_k.shape[0], dtype=jnp.int32)
    allowed = (keys_at[None, :] <= rows_at[:, None]) & (keys_at[None, :] < length)
    one = jnp.einsum("rhd,shd->hrs", first_q, first_k, preferred_element_type=jnp.float32) * scale
    two = jnp.einsum("rhd,shd->hrs", second_q, second_k, preferred_element_type=jnp.float32) * scale
    one = jax.nn.softmax(jnp.where(allowed[None], one, -1e30), axis=-1)
    two = jax.nn.softmax(jnp.where(allowed[None], two, -1e30), axis=-1)
    weights = (one - balance[:, None, None] * two).astype(jnp.bfloat16)
    merged = jnp.einsum("hrs,shv->rhv", weights, values, preferred_element_type=jnp.float32)
    merged = rms_scale(merged, gain[None]) * (1.0 - lambda_base)
    merged = jnp.where((rows_at < length)[:, None, None], merged, 0.0)
    return merged.reshape(merged.shape[0], -1).astype(jnp.bfloat16)


def body(
    tokens,
    lengths,
    positions,
    attn_gain,
    qkv_weight,
    lambdas,
    sub_gain,
    out_weight,
    ffn_gain,
    gate_up_weight,
    down_weight,
):
    prompts_here = lengths.shape[0]
    slots = positions.shape[1]
    width = 4 * HALF + VDIM
    n_head = lax.axis_size("head")
    n_wide = lax.axis_size("wide")
    full_rows = gather_blocks(tokens, "head", n_head, 1)
    normed = rms_scale(full_rows, attn_gain).astype(jnp.bfloat16)
    qkv_local = qkv_weight.astype(jnp.bfloat16)
    qkv_cols = qkv_local.shape[1]
    attn_pack = jnp.concatenate([qkv_local, out_weight.astype(jnp.bfloat16).T], axis=1)
    attn_pack = lax.all_gather(attn_pack, "wide", axis=0, tiled=True)
    gate_up_local = gate_up_weight.astype(jnp.bfloat16)
    gu_shape = gate_up_local.shape
    ffn_pack = jnp.concatenate(
        [gate_up_local.reshape(gu_shape[0], -1), down_weight.astype(jnp.bfloat16).T], axis=1
    )
    ffn_pack = lax.all_gather(ffn_pack, "wide", axis=0, tiled=True)
    columns = normed
    joined = jnp.dot(
        columns,
        attn_pack[:, :qkv_cols],
        preferred_element_type=jnp.float32,
    )
    heads_here = qkv_local.shape[1] // width
    balance = (
        jnp.exp(jnp.sum(lambdas[0] * lambdas[1], -1))
        - jnp.exp(jnp.sum(lambdas[2] * lambdas[3], -1))
        + lambda_base
    )
    outputs = []
    for prompt in range(prompts_here):
        block = joined[prompt * slots : (prompt + 1) * slots].reshape(slots, heads_here, width)
        quads = rotate(
            block[..., : 4 * HALF].reshape(slots, heads_here, 4, HALF), positions[prompt]
        ).astype(jnp.bfloat16)
        values = block[..., 4 * HALF :].astype(jnp.bfloat16)
        length = lengths[prompt]
        first_k = quads[:, :, 2]
        second_k = quads[:, :, 3]
        attended = diff_attend(
            quads[:, :, 0],
            quads[:, :, 1],
            first_k,
            second_k,
            values,
            jnp.arange(slots, dtype=jnp.int32),
            length,
            balance,
            sub_gain,
        )
        outputs.append(attended)
    attn = jnp.concatenate(outputs, axis=0)
    mix_terms = lax.dot_general(
        attn,
        attn_pack[:, qkv_cols:],
        (((1,), (1,)), ((), ())),
        preferred_element_type=jnp.float32,
    )
    mix = scatter_sum(mix_terms, "head", n_head)
    middle = (tokens.astype(jnp.float32) + mix).astype(jnp.bfloat16)
    middle_full = gather_blocks(middle, "head", n_head, 1)
    normed2 = rms_scale(middle_full, ffn_gain).astype(jnp.bfloat16)
    columns = normed2
    gu_cols = gu_shape[1] * gu_shape[2]
    both = jnp.einsum(
        "td,dgf->tgf",
        columns,
        ffn_pack[:, :gu_cols].reshape(-1, gu_shape[1], gu_shape[2]),
        preferred_element_type=jnp.float32,
    )
    hidden = (jax.nn.silu(both[:, 0]) * both[:, 1]).astype(jnp.bfloat16)
    ffn_terms = lax.dot_general(
        hidden,
        ffn_pack[:, gu_cols:],
        (((1,), (1,)), ((), ())),
        preferred_element_type=jnp.float32,
    )
    ffn = scatter_sum(ffn_terms, "head", n_head)
    return (middle.astype(jnp.float32) + ffn).astype(jnp.bfloat16)


def solution(mesh):
    placed = (
        P("wide", "head"),
        P("wide"),
        P("wide", None),
        P(),
        P("wide", "head"),
        P(None, "head", None),
        P("head", None),
        P("head", "wide"),
        P(),
        P("wide", None, "head"),
        P("head", "wide"),
    )
    return jax.shard_map(
        body, mesh=mesh, in_specs=placed, out_specs=P("wide", "head"), check_vma=False
    )
```

```python
import jax
import jax.numpy as jnp
from jax import lax
from jax.sharding import Mesh, PartitionSpec as P

HALF = 128
VDIM = 256


lambda_base = 0.2


def rms_scale(values, gain):
    flat = values.astype(jnp.float32)
    return flat * lax.rsqrt(jnp.mean(flat * flat, axis=-1, keepdims=True) + 1e-05) * gain


def rotate(quads, places):
    width = quads.shape[-1]
    half = width // 2
    freq = 10000.0 ** (-(jnp.arange(half, dtype=jnp.float32) * 2.0 / width))
    angle = places.astype(jnp.float32)[:, None] * freq[None, :]
    cosine = jnp.cos(angle)[:, None, None, :]
    sine = jnp.sin(angle)[:, None, None, :]
    first = quads[..., :half]
    second = quads[..., half:]
    return jnp.concatenate(
        [first * cosine - second * sine, second * cosine + first * sine], axis=-1
    )


def gather_blocks(x, axis, n, dim):
    spread = jnp.broadcast_to(x[None], (n,) + x.shape)
    got = lax.all_to_all(spread, axis, 0, 0, tiled=True)
    got = jnp.moveaxis(got, 0, dim)
    shape = list(x.shape)
    shape[dim] *= n
    return got.reshape(shape)


def scatter_sum(terms, axis, n):
    rows, cols = terms.shape
    parts = terms.astype(jnp.bfloat16).reshape(rows, n, cols // n)
    got = lax.all_to_all(parts, axis, 1, 1, tiled=True)
    return jnp.sum(got.astype(jnp.float32), axis=1)


def gather_weight_rows(pack):
    across = lax.all_gather(pack, "chip", axis=0, tiled=True)
    return lax.all_gather(across, "core", axis=0, tiled=True)


def shard_order(values, n_wide):
    rows, cols = values.shape
    split = values.reshape(rows, n_wide // 2, 2, cols // n_wide)
    return jnp.swapaxes(split, 1, 2).reshape(rows, cols)


def feature_order(values, n_wide):
    rows, cols = values.shape
    split = values.reshape(rows, 2, n_wide // 2, cols // n_wide)
    return jnp.swapaxes(split, 1, 2).reshape(rows, cols)


def diff_attend(first_q, second_q, first_k, second_k, values, rows_at, length, balance, gain):
    scale = first_q.shape[-1] ** (-0.5)
    keys_at = jnp.arange(first_k.shape[0], dtype=jnp.int32)
    allowed = (keys_at[None, :] <= rows_at[:, None]) & (keys_at[None, :] < length)
    one = jnp.einsum("rhd,shd->hrs", first_q, first_k, preferred_element_type=jnp.float32) * scale
    two = jnp.einsum("rhd,shd->hrs", second_q, second_k, preferred_element_type=jnp.float32) * scale
    one = jax.nn.softmax(jnp.where(allowed[None], one, -1e30), axis=-1)
    two = jax.nn.softmax(jnp.where(allowed[None], two, -1e30), axis=-1)
    weights = (one - balance[:, None, None] * two).astype(jnp.bfloat16)
    merged = jnp.einsum("hrs,shv->rhv", weights, values, preferred_element_type=jnp.float32)
    merged = rms_scale(merged, gain[None]) * (1.0 - lambda_base)
    merged = jnp.where((rows_at < length)[:, None, None], merged, 0.0)
    return merged.reshape(merged.shape[0], -1).astype(jnp.bfloat16)


def body(
    tokens,
    lengths,
    positions,
    attn_gain,
    qkv_weight,
    lambdas,
    sub_gain,
    out_weight,
    ffn_gain,
    gate_up_weight,
    down_weight,
):
    prompts_here = lengths.shape[0]
    slots = positions.shape[1]
    width = 4 * HALF + VDIM
    n_head = lax.axis_size("head")
    n_wide = lax.axis_size("chip") * lax.axis_size("core")
    full_rows = gather_blocks(tokens, "head", n_head, 1)
    normed = rms_scale(full_rows, attn_gain).astype(jnp.bfloat16)
    qkv_local = qkv_weight.astype(jnp.bfloat16)
    qkv_cols = qkv_local.shape[1]
    attn_pack = jnp.concatenate([qkv_local, out_weight.astype(jnp.bfloat16).T], axis=1)
    attn_pack = gather_weight_rows(attn_pack)
    gate_up_local = gate_up_weight.astype(jnp.bfloat16)
    gu_shape = gate_up_local.shape
    ffn_pack = jnp.concatenate(
        [gate_up_local.reshape(gu_shape[0], -1), down_weight.astype(jnp.bfloat16).T], axis=1
    )
    ffn_pack = gather_weight_rows(ffn_pack)
    columns = shard_order(normed, n_wide)
    joined = jnp.dot(
        columns,
        attn_pack[:, :qkv_cols],
        preferred_element_type=jnp.float32,
    )
    heads_here = qkv_local.shape[1] // width
    balance = (
        jnp.exp(jnp.sum(lambdas[0] * lambdas[1], -1))
        - jnp.exp(jnp.sum(lambdas[2] * lambdas[3], -1))
        + lambda_base
    )
    outputs = []
    for prompt in range(prompts_here):
        block = joined[prompt * slots : (prompt + 1) * slots].reshape(slots, heads_here, width)
        quads = rotate(
            block[..., : 4 * HALF].reshape(slots, heads_here, 4, HALF), positions[prompt]
        ).astype(jnp.bfloat16)
        values = block[..., 4 * HALF :].astype(jnp.bfloat16)
        length = lengths[prompt]
        first_k = quads[:, :, 2]
        second_k = quads[:, :, 3]
        attended = diff_attend(
            quads[:, :, 0],
            quads[:, :, 1],
            first_k,
            second_k,
            values,
            jnp.arange(slots, dtype=jnp.int32),
            length,
            balance,
            sub_gain,
        )
        outputs.append(attended)
    attn = jnp.concatenate(outputs, axis=0)
    mix_terms = lax.dot_general(
        attn,
        attn_pack[:, qkv_cols:],
        (((1,), (1,)), ((), ())),
        preferred_element_type=jnp.float32,
    )
    mix = scatter_sum(feature_order(mix_terms, n_wide), "head", n_head)
    middle = (tokens.astype(jnp.float32) + mix).astype(jnp.bfloat16)
    middle_full = gather_blocks(middle, "head", n_head, 1)
    normed2 = rms_scale(middle_full, ffn_gain).astype(jnp.bfloat16)
    columns = shard_order(normed2, n_wide)
    gu_cols = gu_shape[1] * gu_shape[2]
    both = jnp.einsum(
        "td,dgf->tgf",
        columns,
        ffn_pack[:, :gu_cols].reshape(-1, gu_shape[1], gu_shape[2]),
        preferred_element_type=jnp.float32,
    )
    hidden = (jax.nn.silu(both[:, 0]) * both[:, 1]).astype(jnp.bfloat16)
    ffn_terms = lax.dot_general(
        hidden,
        ffn_pack[:, gu_cols:],
        (((1,), (1,)), ((), ())),
        preferred_element_type=jnp.float32,
    )
    ffn = scatter_sum(feature_order(ffn_terms, n_wide), "head", n_head)
    return (middle.astype(jnp.float32) + ffn).astype(jnp.bfloat16)


def solution(mesh):
    n_wide = mesh.shape["wide"]
    n_head = mesh.shape["head"]
    fine = Mesh(mesh.devices.reshape(n_wide // 2, 2, n_head), ("chip", "core", "head"))
    wide = ("chip", "core")
    placed = (
        P(wide, "head"),
        P(wide),
        P(wide, None),
        P(),
        P(wide, "head"),
        P(None, "head", None),
        P("head", None),
        P("head", wide),
        P(),
        P(wide, None, "head"),
        P("head", wide),
    )
    return jax.shard_map(
        body, mesh=fine, in_specs=placed, out_specs=P(wide, "head"), check_vma=False
    )
```

```python
import jax
import jax.numpy as jnp
from jax import lax
from jax.sharding import PartitionSpec as P

HALF = 128
VDIM = 256


lambda_base = 0.2


def rms_scale(values, gain):
    flat = values.astype(jnp.float32)
    return flat * lax.rsqrt(jnp.mean(flat * flat, axis=-1, keepdims=True) + 1e-05) * gain


def rotate(quads, places):
    width = quads.shape[-1]
    half = width // 2
    freq = 10000.0 ** (-(jnp.arange(half, dtype=jnp.float32) * 2.0 / width))
    angle = places.astype(jnp.float32)[:, None] * freq[None, :]
    cosine = jnp.cos(angle)[:, None, None, :]
    sine = jnp.sin(angle)[:, None, None, :]
    first = quads[..., :half]
    second = quads[..., half:]
    return jnp.concatenate(
        [first * cosine - second * sine, second * cosine + first * sine], axis=-1
    )


def gather_blocks(x, axis, n, dim):
    spread = jnp.broadcast_to(x[None], (n,) + x.shape)
    got = lax.all_to_all(spread, axis, 0, 0, tiled=True)
    got = jnp.moveaxis(got, 0, dim)
    shape = list(x.shape)
    shape[dim] *= n
    return got.reshape(shape)


def scatter_sum(terms, axis, n):
    rows, cols = terms.shape
    parts = terms.astype(jnp.bfloat16).reshape(rows, n, cols // n)
    got = lax.all_to_all(parts, axis, 1, 1, tiled=True)
    return jnp.sum(got.astype(jnp.float32), axis=1)


def diff_attend(first_q, second_q, first_k, second_k, values, rows_at, length, balance, gain):
    scale = first_q.shape[-1] ** (-0.5)
    keys_at = jnp.arange(first_k.shape[0], dtype=jnp.int32)
    allowed = (keys_at[None, :] <= rows_at[:, None]) & (keys_at[None, :] < length)
    one = jnp.einsum("rhd,shd->hrs", first_q, first_k, preferred_element_type=jnp.float32) * scale
    two = jnp.einsum("rhd,shd->hrs", second_q, second_k, preferred_element_type=jnp.float32) * scale
    one = jax.nn.softmax(jnp.where(allowed[None], one, -1e30), axis=-1)
    two = jax.nn.softmax(jnp.where(allowed[None], two, -1e30), axis=-1)
    weights = (one - balance[:, None, None] * two).astype(jnp.bfloat16)
    merged = jnp.einsum("hrs,shv->rhv", weights, values, preferred_element_type=jnp.float32)
    merged = rms_scale(merged, gain[None]) * (1.0 - lambda_base)
    merged = jnp.where((rows_at < length)[:, None, None], merged, 0.0)
    return merged.reshape(merged.shape[0], -1).astype(jnp.bfloat16)


def body(
    tokens,
    lengths,
    positions,
    attn_gain,
    qkv_weight,
    lambdas,
    sub_gain,
    out_weight,
    ffn_gain,
    gate_up_weight,
    down_weight,
):
    prompts_here = lengths.shape[0]
    slots = positions.shape[1]
    width = 4 * HALF + VDIM
    n_head = lax.axis_size("head")
    qkv_local = qkv_weight.astype(jnp.bfloat16)
    qkv_cols = qkv_local.shape[1]
    heads_here = qkv_cols // width
    attn_pack = jnp.concatenate([qkv_local, out_weight.astype(jnp.bfloat16).T], axis=1)
    attn_pack = lax.all_gather(attn_pack, "wide", axis=0, tiled=True)
    gate_up_local = gate_up_weight.astype(jnp.bfloat16)
    gu_shape = gate_up_local.shape
    gu_cols = gu_shape[1] * gu_shape[2]
    ffn_pack = jnp.concatenate(
        [gate_up_local.reshape(gu_shape[0], -1), down_weight.astype(jnp.bfloat16).T], axis=1
    )
    ffn_pack = lax.all_gather(ffn_pack, "wide", axis=0, tiled=True)
    balance = (
        jnp.exp(jnp.sum(lambdas[0] * lambdas[1], -1))
        - jnp.exp(jnp.sum(lambdas[2] * lambdas[3], -1))
        + lambda_base
    )
    results = []
    for prompt in range(prompts_here):
        stream = tokens[prompt * slots : (prompt + 1) * slots]
        full_rows = gather_blocks(stream, "head", n_head, 1)
        normed = rms_scale(full_rows, attn_gain).astype(jnp.bfloat16)
        joined = jnp.dot(normed, attn_pack[:, :qkv_cols], preferred_element_type=jnp.float32)
        block = joined.reshape(slots, heads_here, width)
        quads = rotate(
            block[..., : 4 * HALF].reshape(slots, heads_here, 4, HALF), positions[prompt]
        ).astype(jnp.bfloat16)
        values = block[..., 4 * HALF :].astype(jnp.bfloat16)
        attn = diff_attend(
            quads[:, :, 0],
            quads[:, :, 1],
            quads[:, :, 2],
            quads[:, :, 3],
            values,
            jnp.arange(slots, dtype=jnp.int32),
            lengths[prompt],
            balance,
            sub_gain,
        )
        mix_terms = lax.dot_general(
            attn,
            attn_pack[:, qkv_cols:],
            (((1,), (1,)), ((), ())),
            preferred_element_type=jnp.float32,
        )
        mix = scatter_sum(mix_terms, "head", n_head)
        middle = (stream.astype(jnp.float32) + mix).astype(jnp.bfloat16)
        middle_full = gather_blocks(middle, "head", n_head, 1)
        normed2 = rms_scale(middle_full, ffn_gain).astype(jnp.bfloat16)
        both = jnp.einsum(
            "td,dgf->tgf",
            normed2,
            ffn_pack[:, :gu_cols].reshape(-1, gu_shape[1], gu_shape[2]),
            preferred_element_type=jnp.float32,
        )
        hidden = (jax.nn.silu(both[:, 0]) * both[:, 1]).astype(jnp.bfloat16)
        ffn_terms = lax.dot_general(
            hidden,
            ffn_pack[:, gu_cols:],
            (((1,), (1,)), ((), ())),
            preferred_element_type=jnp.float32,
        )
        ffn = scatter_sum(ffn_terms, "head", n_head)
        results.append((middle.astype(jnp.float32) + ffn).astype(jnp.bfloat16))
    return jnp.concatenate(results, axis=0)


def solution(mesh):
    placed = (
        P("wide", "head"),
        P("wide"),
        P("wide", None),
        P(),
        P("wide", "head"),
        P(None, "head", None),
        P("head", None),
        P("head", "wide"),
        P(),
        P("wide", None, "head"),
        P("head", "wide"),
    )
    return jax.shard_map(
        body, mesh=mesh, in_specs=placed, out_specs=P("wide", "head"), check_vma=False
    )
```

```python
import jax
import jax.numpy as jnp
from jax import lax
from jax.sharding import Mesh, PartitionSpec as P

HALF = 128
VDIM = 256


lambda_base = 0.2


def rms_scale(values, gain):
    flat = values.astype(jnp.float32)
    return flat * lax.rsqrt(jnp.mean(flat * flat, axis=-1, keepdims=True) + 1e-05) * gain


def rotate(quads, places):
    width = quads.shape[-1]
    half = width // 2
    freq = 10000.0 ** (-(jnp.arange(half, dtype=jnp.float32) * 2.0 / width))
    angle = places.astype(jnp.float32)[:, None] * freq[None, :]
    cosine = jnp.cos(angle)[:, None, None, :]
    sine = jnp.sin(angle)[:, None, None, :]
    first = quads[..., :half]
    second = quads[..., half:]
    return jnp.concatenate(
        [first * cosine - second * sine, second * cosine + first * sine], axis=-1
    )


def gather_blocks(x, axis, n, dim):
    spread = jnp.broadcast_to(x[None], (n,) + x.shape)
    got = lax.all_to_all(spread, axis, 0, 0, tiled=True)
    got = jnp.moveaxis(got, 0, dim)
    shape = list(x.shape)
    shape[dim] *= n
    return got.reshape(shape)


def scatter_sum(terms, axis, n):
    rows, cols = terms.shape
    parts = terms.astype(jnp.bfloat16).reshape(rows, n, cols // n)
    got = lax.all_to_all(parts, axis, 1, 1, tiled=True)
    return jnp.sum(got.astype(jnp.float32), axis=1)


def gather_weight_rows(pack):
    rows, cols = pack.shape
    across = lax.all_gather(pack, "chip", axis=0, tiled=True)
    both = lax.all_gather(across, "core", axis=0, tiled=True)
    cores = lax.axis_size("core")
    split = both.reshape(cores, -1, rows, cols)
    return jnp.swapaxes(split, 0, 1).reshape(-1, cols)


def diff_attend(first_q, second_q, first_k, second_k, values, rows_at, length, balance, gain):
    scale = first_q.shape[-1] ** (-0.5)
    keys_at = jnp.arange(first_k.shape[0], dtype=jnp.int32)
    allowed = (keys_at[None, :] <= rows_at[:, None]) & (keys_at[None, :] < length)
    one = jnp.einsum("rhd,shd->hrs", first_q, first_k, preferred_element_type=jnp.float32) * scale
    two = jnp.einsum("rhd,shd->hrs", second_q, second_k, preferred_element_type=jnp.float32) * scale
    one = jax.nn.softmax(jnp.where(allowed[None], one, -1e30), axis=-1)
    two = jax.nn.softmax(jnp.where(allowed[None], two, -1e30), axis=-1)
    weights = (one - balance[:, None, None] * two).astype(jnp.bfloat16)
    merged = jnp.einsum("hrs,shv->rhv", weights, values, preferred_element_type=jnp.float32)
    merged = rms_scale(merged, gain[None]) * (1.0 - lambda_base)
    merged = jnp.where((rows_at < length)[:, None, None], merged, 0.0)
    return merged.reshape(merged.shape[0], -1).astype(jnp.bfloat16)


def body(
    tokens,
    lengths,
    positions,
    attn_gain,
    qkv_weight,
    lambdas,
    sub_gain,
    out_weight,
    ffn_gain,
    gate_up_weight,
    down_weight,
):
    prompts_here = lengths.shape[0]
    slots = positions.shape[1]
    width = 4 * HALF + VDIM
    n_head = lax.axis_size("head")
    full_rows = gather_blocks(tokens, "head", n_head, 1)
    normed = rms_scale(full_rows, attn_gain).astype(jnp.bfloat16)
    qkv_local = qkv_weight.astype(jnp.bfloat16)
    qkv_cols = qkv_local.shape[1]
    attn_pack = jnp.concatenate([qkv_local, out_weight.astype(jnp.bfloat16).T], axis=1)
    attn_pack = lax.all_gather(attn_pack, ("chip", "core"), axis=0, tiled=True)
    gate_up_local = gate_up_weight.astype(jnp.bfloat16)
    gu_shape = gate_up_local.shape
    ffn_pack = jnp.concatenate(
        [gate_up_local.reshape(gu_shape[0], -1), down_weight.astype(jnp.bfloat16).T], axis=1
    )
    ffn_pack = gather_weight_rows(ffn_pack)
    columns = normed
    joined = jnp.dot(
        columns,
        attn_pack[:, :qkv_cols],
        preferred_element_type=jnp.float32,
    )
    heads_here = qkv_local.shape[1] // width
    balance = (
        jnp.exp(jnp.sum(lambdas[0] * lambdas[1], -1))
        - jnp.exp(jnp.sum(lambdas[2] * lambdas[3], -1))
        + lambda_base
    )
    outputs = []
    for prompt in range(prompts_here):
        block = joined[prompt * slots : (prompt + 1) * slots].reshape(slots, heads_here, width)
        quads = rotate(
            block[..., : 4 * HALF].reshape(slots, heads_here, 4, HALF), positions[prompt]
        ).astype(jnp.bfloat16)
        values = block[..., 4 * HALF :].astype(jnp.bfloat16)
        length = lengths[prompt]
        first_k = quads[:, :, 2]
        second_k = quads[:, :, 3]
        attended = diff_attend(
            quads[:, :, 0],
            quads[:, :, 1],
            first_k,
            second_k,
            values,
            jnp.arange(slots, dtype=jnp.int32),
            length,
            balance,
            sub_gain,
        )
        outputs.append(attended)
    attn = jnp.concatenate(outputs, axis=0)
    mix_terms = lax.dot_general(
        attn,
        attn_pack[:, qkv_cols:],
        (((1,), (1,)), ((), ())),
        preferred_element_type=jnp.float32,
    )
    mix = scatter_sum(mix_terms, "head", n_head)
    middle = (tokens.astype(jnp.float32) + mix).astype(jnp.bfloat16)
    middle_full = gather_blocks(middle, "head", n_head, 1)
    normed2 = rms_scale(middle_full, ffn_gain).astype(jnp.bfloat16)
    columns = normed2
    gu_cols = gu_shape[1] * gu_shape[2]
    both = jnp.einsum(
        "td,dgf->tgf",
        columns,
        ffn_pack[:, :gu_cols].reshape(-1, gu_shape[1], gu_shape[2]),
        preferred_element_type=jnp.float32,
    )
    hidden = (jax.nn.silu(both[:, 0]) * both[:, 1]).astype(jnp.bfloat16)
    ffn_terms = lax.dot_general(
        hidden,
        ffn_pack[:, gu_cols:],
        (((1,), (1,)), ((), ())),
        preferred_element_type=jnp.float32,
    )
    ffn = scatter_sum(ffn_terms, "head", n_head)
    return (middle.astype(jnp.float32) + ffn).astype(jnp.bfloat16)


def solution(mesh):
    n_wide = mesh.shape["wide"]
    n_head = mesh.shape["head"]
    fine = Mesh(mesh.devices.reshape(n_wide // 2, 2, n_head), ("chip", "core", "head"))
    wide = ("chip", "core")
    placed = (
        P(wide, "head"),
        P(wide),
        P(wide, None),
        P(),
        P(wide, "head"),
        P(None, "head", None),
        P("head", None),
        P("head", wide),
        P(),
        P(wide, None, "head"),
        P("head", wide),
    )
    return jax.shard_map(
        body, mesh=fine, in_specs=placed, out_specs=P(wide, "head"), check_vma=False
    )
```

```python
import jax
import jax.numpy as jnp
from jax import lax
from jax.sharding import PartitionSpec as P

HALF = 128
VDIM = 256


lambda_base = 0.2


def rms_scale(values, gain):
    flat = values.astype(jnp.float32)
    return flat * lax.rsqrt(jnp.mean(flat * flat, axis=-1, keepdims=True) + 1e-05) * gain


def rotate(quads, places):
    width = quads.shape[-1]
    half = width // 2
    freq = 10000.0 ** (-(jnp.arange(half, dtype=jnp.float32) * 2.0 / width))
    angle = places.astype(jnp.float32)[:, None] * freq[None, :]
    cosine = jnp.cos(angle)[:, None, None, :]
    sine = jnp.sin(angle)[:, None, None, :]
    first = quads[..., :half]
    second = quads[..., half:]
    return jnp.concatenate(
        [first * cosine - second * sine, second * cosine + first * sine], axis=-1
    )


def gather_blocks(x, axis, n, dim):
    spread = jnp.broadcast_to(x[None], (n,) + x.shape)
    got = lax.all_to_all(spread, axis, 0, 0, tiled=True)
    got = jnp.moveaxis(got, 0, dim)
    shape = list(x.shape)
    shape[dim] *= n
    return got.reshape(shape)


def scatter_sum(terms, axis, n):
    rows, cols = terms.shape
    parts = terms.astype(jnp.bfloat16).reshape(rows, n, cols // n)
    got = lax.all_to_all(parts, axis, 1, 1, tiled=True)
    return jnp.sum(got.astype(jnp.float32), axis=1)


def diff_attend(first_q, second_q, first_k, second_k, values, rows_at, length, balance, gain):
    scale = first_q.shape[-1] ** (-0.5)
    keys_at = jnp.arange(first_k.shape[0], dtype=jnp.int32)
    allowed = (keys_at[None, :] <= rows_at[:, None]) & (keys_at[None, :] < length)
    one = jnp.einsum("rhd,shd->hrs", first_q, first_k, preferred_element_type=jnp.float32) * scale
    two = jnp.einsum("rhd,shd->hrs", second_q, second_k, preferred_element_type=jnp.float32) * scale
    one = jax.nn.softmax(jnp.where(allowed[None], one, -1e30), axis=-1)
    two = jax.nn.softmax(jnp.where(allowed[None], two, -1e30), axis=-1)
    weights = (one - balance[:, None, None] * two).astype(jnp.bfloat16)
    merged = jnp.einsum("hrs,shv->rhv", weights, values, preferred_element_type=jnp.float32)
    merged = rms_scale(merged, gain[None]) * (1.0 - lambda_base)
    merged = jnp.where((rows_at < length)[:, None, None], merged, 0.0)
    return merged.reshape(merged.shape[0], -1).astype(jnp.bfloat16)


def body(
    tokens,
    lengths,
    positions,
    attn_gain,
    qkv_weight,
    lambdas,
    sub_gain,
    out_weight,
    ffn_gain,
    gate_up_weight,
    down_weight,
):
    prompts_here = lengths.shape[0]
    slots = positions.shape[1]
    width = 4 * HALF + VDIM
    n_head = lax.axis_size("head")
    n_wide = lax.axis_size("wide")
    full_rows = gather_blocks(tokens, "head", n_head, 1)
    normed = rms_scale(full_rows, attn_gain).astype(jnp.bfloat16)
    qkv_local = qkv_weight.astype(jnp.bfloat16)
    qkv_cols = qkv_local.shape[1]
    attn_pack = jnp.concatenate([qkv_local, out_weight.astype(jnp.bfloat16).T], axis=1)
    attn_pack = lax.all_gather(attn_pack, "wide", axis=0, tiled=True)
    gate_up_local = gate_up_weight.astype(jnp.bfloat16)
    gu_shape = gate_up_local.shape
    ffn_pack = jnp.concatenate(
        [gate_up_local.reshape(gu_shape[0], -1), down_weight.astype(jnp.bfloat16).T], axis=1
    )
    ffn_pack = lax.all_gather(ffn_pack, "wide", axis=0, tiled=True)
    columns = normed
    joined = jnp.dot(
        columns,
        attn_pack[:, :qkv_cols],
        preferred_element_type=jnp.float32,
    )
    heads_here = qkv_local.shape[1] // width
    balance = (
        jnp.exp(jnp.sum(lambdas[0] * lambdas[1], -1))
        - jnp.exp(jnp.sum(lambdas[2] * lambdas[3], -1))
        + lambda_base
    )
    outputs = []
    for prompt in range(prompts_here):
        block = joined[prompt * slots : (prompt + 1) * slots].reshape(slots, heads_here, width)
        quads = rotate(
            block[..., : 4 * HALF].reshape(slots, heads_here, 4, HALF), positions[prompt]
        ).astype(jnp.bfloat16)
        values = block[..., 4 * HALF :].astype(jnp.bfloat16)
        length = lengths[prompt]
        first_k = quads[:, :, 2]
        second_k = quads[:, :, 3]
        attended = diff_attend(
            quads[:, :, 0],
            quads[:, :, 1],
            first_k,
            second_k,
            values,
            jnp.arange(slots, dtype=jnp.int32),
            length,
            balance,
            sub_gain,
        )
        outputs.append(attended)
    attn = jnp.concatenate(outputs, axis=0)
    mix_terms = lax.dot_general(
        attn,
        attn_pack[:, qkv_cols:],
        (((1,), (1,)), ((), ())),
        preferred_element_type=jnp.float32,
    )
    mix = scatter_sum(mix_terms, "head", n_head)
    middle = (tokens.astype(jnp.float32) + mix).astype(jnp.bfloat16)
    middle_cols = gather_blocks(middle.T, "head", n_head, 0)
    flat = middle_cols.astype(jnp.float32)
    scale = lax.rsqrt(jnp.mean(flat * flat, axis=0, keepdims=True) + 1e-05)
    normed2 = (flat * scale * ffn_gain[:, None]).astype(jnp.bfloat16)
    columns = normed2
    gu_cols = gu_shape[1] * gu_shape[2]
    both = jnp.einsum(
        "dt,dgf->tgf",
        columns,
        ffn_pack[:, :gu_cols].reshape(-1, gu_shape[1], gu_shape[2]),
        preferred_element_type=jnp.float32,
    )
    hidden = (jax.nn.silu(both[:, 0]) * both[:, 1]).astype(jnp.bfloat16)
    ffn_terms = lax.dot_general(
        hidden,
        ffn_pack[:, gu_cols:],
        (((1,), (1,)), ((), ())),
        preferred_element_type=jnp.float32,
    )
    ffn = scatter_sum(ffn_terms, "head", n_head)
    return (middle.astype(jnp.float32) + ffn).astype(jnp.bfloat16)


def solution(mesh):
    placed = (
        P("wide", "head"),
        P("wide"),
        P("wide", None),
        P(),
        P("wide", "head"),
        P(None, "head", None),
        P("head", None),
        P("head", "wide"),
        P(),
        P("wide", None, "head"),
        P("head", "wide"),
    )
    return jax.shard_map(
        body, mesh=mesh, in_specs=placed, out_specs=P("wide", "head"), check_vma=False
    )
```

```python
import jax
import jax.numpy as jnp
from jax import lax
from jax.sharding import PartitionSpec as P

HALF = 128
VDIM = 256


lambda_base = 0.2


def rms_scale(values, gain):
    flat = values.astype(jnp.float32)
    return flat * lax.rsqrt(jnp.mean(flat * flat, axis=-1, keepdims=True) + 1e-05) * gain


def rotate(quads, places):
    width = quads.shape[-1]
    half = width // 2
    freq = 10000.0 ** (-(jnp.arange(half, dtype=jnp.float32) * 2.0 / width))
    angle = places.astype(jnp.float32)[:, None] * freq[None, :]
    cosine = jnp.cos(angle)[:, None, None, :]
    sine = jnp.sin(angle)[:, None, None, :]
    first = quads[..., :half]
    second = quads[..., half:]
    return jnp.concatenate(
        [first * cosine - second * sine, second * cosine + first * sine], axis=-1
    )


def gather_blocks(x, axis, n, dim):
    spread = jnp.broadcast_to(x[None], (n,) + x.shape)
    got = lax.all_to_all(spread, axis, 0, 0, tiled=True)
    got = jnp.moveaxis(got, 0, dim)
    shape = list(x.shape)
    shape[dim] *= n
    return got.reshape(shape)


def scatter_sum(terms, axis, n):
    rows, cols = terms.shape
    parts = terms.astype(jnp.bfloat16).reshape(rows, n, cols // n)
    got = lax.all_to_all(parts, axis, 1, 1, tiled=True)
    return jnp.sum(got.astype(jnp.float32), axis=1)


def gather_rows_shifted(pack, axis, n):
    me = lax.axis_index(axis)
    pieces = [pack]
    for shift in range(1, n):
        pairs = [((i + shift) % n, i) for i in range(n)]
        pieces.append(lax.ppermute(pack, axis, pairs))
    stacked = jnp.roll(jnp.stack(pieces), me, axis=0)
    return stacked.reshape(n * pack.shape[0], pack.shape[1])


def diff_attend(first_q, second_q, first_k, second_k, values, rows_at, length, balance, gain):
    scale = first_q.shape[-1] ** (-0.5)
    keys_at = jnp.arange(first_k.shape[0], dtype=jnp.int32)
    allowed = (keys_at[None, :] <= rows_at[:, None]) & (keys_at[None, :] < length)
    one = jnp.einsum("rhd,shd->hrs", first_q, first_k, preferred_element_type=jnp.float32) * scale
    two = jnp.einsum("rhd,shd->hrs", second_q, second_k, preferred_element_type=jnp.float32) * scale
    one = jax.nn.softmax(jnp.where(allowed[None], one, -1e30), axis=-1)
    two = jax.nn.softmax(jnp.where(allowed[None], two, -1e30), axis=-1)
    weights = (one - balance[:, None, None] * two).astype(jnp.bfloat16)
    merged = jnp.einsum("hrs,shv->rhv", weights, values, preferred_element_type=jnp.float32)
    merged = rms_scale(merged, gain[None]) * (1.0 - lambda_base)
    merged = jnp.where((rows_at < length)[:, None, None], merged, 0.0)
    return merged.reshape(merged.shape[0], -1).astype(jnp.bfloat16)


def body(
    tokens,
    lengths,
    positions,
    attn_gain,
    qkv_weight,
    lambdas,
    sub_gain,
    out_weight,
    ffn_gain,
    gate_up_weight,
    down_weight,
):
    prompts_here = lengths.shape[0]
    slots = positions.shape[1]
    width = 4 * HALF + VDIM
    n_head = lax.axis_size("head")
    n_wide = lax.axis_size("wide")
    full_rows = gather_blocks(tokens, "head", n_head, 1)
    normed = rms_scale(full_rows, attn_gain).astype(jnp.bfloat16)
    qkv_local = qkv_weight.astype(jnp.bfloat16)
    qkv_cols = qkv_local.shape[1]
    attn_pack = jnp.concatenate([qkv_local, out_weight.astype(jnp.bfloat16).T], axis=1)
    attn_pack = gather_rows_shifted(attn_pack, "wide", lax.axis_size("wide"))
    gate_up_local = gate_up_weight.astype(jnp.bfloat16)
    gu_shape = gate_up_local.shape
    ffn_pack = jnp.concatenate(
        [gate_up_local.reshape(gu_shape[0], -1), down_weight.astype(jnp.bfloat16).T], axis=1
    )
    ffn_pack = gather_rows_shifted(ffn_pack, "wide", lax.axis_size("wide"))
    columns = normed
    joined = jnp.dot(
        columns,
        attn_pack[:, :qkv_cols],
        preferred_element_type=jnp.float32,
    )
    heads_here = qkv_local.shape[1] // width
    balance = (
        jnp.exp(jnp.sum(lambdas[0] * lambdas[1], -1))
        - jnp.exp(jnp.sum(lambdas[2] * lambdas[3], -1))
        + lambda_base
    )
    outputs = []
    for prompt in range(prompts_here):
        block = joined[prompt * slots : (prompt + 1) * slots].reshape(slots, heads_here, width)
        quads = rotate(
            block[..., : 4 * HALF].reshape(slots, heads_here, 4, HALF), positions[prompt]
        ).astype(jnp.bfloat16)
        values = block[..., 4 * HALF :].astype(jnp.bfloat16)
        length = lengths[prompt]
        first_k = quads[:, :, 2]
        second_k = quads[:, :, 3]
        attended = diff_attend(
            quads[:, :, 0],
            quads[:, :, 1],
            first_k,
            second_k,
            values,
            jnp.arange(slots, dtype=jnp.int32),
            length,
            balance,
            sub_gain,
        )
        outputs.append(attended)
    attn = jnp.concatenate(outputs, axis=0)
    mix_terms = lax.dot_general(
        attn,
        attn_pack[:, qkv_cols:],
        (((1,), (1,)), ((), ())),
        preferred_element_type=jnp.float32,
    )
    mix = scatter_sum(mix_terms, "head", n_head)
    middle = (tokens.astype(jnp.float32) + mix).astype(jnp.bfloat16)
    middle_cols = gather_blocks(middle.T, "head", n_head, 0)
    flat = middle_cols.astype(jnp.float32)
    scale = lax.rsqrt(jnp.mean(flat * flat, axis=0, keepdims=True) + 1e-05)
    normed2 = (flat * scale * ffn_gain[:, None]).astype(jnp.bfloat16)
    columns = normed2
    gu_cols = gu_shape[1] * gu_shape[2]
    both = jnp.einsum(
        "dt,dgf->tgf",
        columns,
        ffn_pack[:, :gu_cols].reshape(-1, gu_shape[1], gu_shape[2]),
        preferred_element_type=jnp.float32,
    )
    hidden = (jax.nn.silu(both[:, 0]) * both[:, 1]).astype(jnp.bfloat16)
    ffn_terms = lax.dot_general(
        hidden,
        ffn_pack[:, gu_cols:],
        (((1,), (1,)), ((), ())),
        preferred_element_type=jnp.float32,
    )
    ffn = scatter_sum(ffn_terms, "head", n_head)
    return (middle.astype(jnp.float32) + ffn).astype(jnp.bfloat16)


def solution(mesh):
    placed = (
        P("wide", "head"),
        P("wide"),
        P("wide", None),
        P(),
        P("wide", "head"),
        P(None, "head", None),
        P("head", None),
        P("head", "wide"),
        P(),
        P("wide", None, "head"),
        P("head", "wide"),
    )
    return jax.shard_map(
        body, mesh=mesh, in_specs=placed, out_specs=P("wide", "head"), check_vma=False
    )
```

```python
import jax
import jax.numpy as jnp
from jax import lax
from jax.sharding import PartitionSpec as P

HALF = 128
VDIM = 256


lambda_base = 0.2


def rms_scale(values, gain):
    flat = values.astype(jnp.float32)
    return flat * lax.rsqrt(jnp.mean(flat * flat, axis=-1, keepdims=True) + 1e-05) * gain


def rotate(quads, places):
    width = quads.shape[-1]
    half = width // 2
    freq = 10000.0 ** (-(jnp.arange(half, dtype=jnp.float32) * 2.0 / width))
    angle = places.astype(jnp.float32)[:, None] * freq[None, :]
    cosine = jnp.cos(angle)[:, None, None, :]
    sine = jnp.sin(angle)[:, None, None, :]
    first = quads[..., :half]
    second = quads[..., half:]
    return jnp.concatenate(
        [first * cosine - second * sine, second * cosine + first * sine], axis=-1
    )


def gather_blocks(x, axis, n, dim):
    spread = jnp.broadcast_to(x[None], (n,) + x.shape)
    got = lax.all_to_all(spread, axis, 0, 0, tiled=True)
    got = jnp.moveaxis(got, 0, dim)
    shape = list(x.shape)
    shape[dim] *= n
    return got.reshape(shape)


def scatter_sum(terms, axis, n):
    rows, cols = terms.shape
    parts = terms.astype(jnp.bfloat16).reshape(rows, n, cols // n)
    got = lax.all_to_all(parts, axis, 1, 1, tiled=True)
    return jnp.sum(got.astype(jnp.float32), axis=1)


def diff_attend(first_q, second_q, first_k, second_k, values, rows_at, length, balance, gain):
    scale = first_q.shape[-1] ** (-0.5)
    keys_at = jnp.arange(first_k.shape[0], dtype=jnp.int32)
    allowed = (keys_at[None, :] <= rows_at[:, None]) & (keys_at[None, :] < length)
    one = jnp.einsum("rhd,shd->hrs", first_q, first_k, preferred_element_type=jnp.float32) * scale
    two = jnp.einsum("rhd,shd->hrs", second_q, second_k, preferred_element_type=jnp.float32) * scale
    one = jax.nn.softmax(jnp.where(allowed[None], one, -1e30), axis=-1)
    two = jax.nn.softmax(jnp.where(allowed[None], two, -1e30), axis=-1)
    weights = (one - balance[:, None, None] * two).astype(jnp.bfloat16)
    merged = jnp.einsum("hrs,shv->rhv", weights, values, preferred_element_type=jnp.float32)
    merged = rms_scale(merged, gain[None]) * (1.0 - lambda_base)
    merged = jnp.where((rows_at < length)[:, None, None], merged, 0.0)
    return merged.reshape(merged.shape[0], -1).astype(jnp.bfloat16)


def body(
    tokens,
    lengths,
    positions,
    attn_gain,
    qkv_weight,
    lambdas,
    sub_gain,
    out_weight,
    ffn_gain,
    gate_up_weight,
    down_weight,
):
    prompts_here = lengths.shape[0]
    slots = positions.shape[1]
    width = 4 * HALF + VDIM
    n_head = lax.axis_size("head")
    n_wide = lax.axis_size("wide")
    full_rows = gather_blocks(tokens, "head", n_head, 1)
    normed = rms_scale(full_rows, attn_gain).astype(jnp.bfloat16)
    qkv_local = qkv_weight.astype(jnp.bfloat16)
    qkv_cols = qkv_local.shape[1]
    attn_pack = jnp.concatenate([qkv_local, out_weight.astype(jnp.bfloat16).T], axis=1)
    attn_pack = lax.all_gather(attn_pack, "wide", axis=0, tiled=True)
    gate_up_local = gate_up_weight.astype(jnp.bfloat16)
    gu_shape = gate_up_local.shape
    ffn_pack = jnp.concatenate(
        [gate_up_local.reshape(gu_shape[0], -1), down_weight.astype(jnp.bfloat16).T], axis=1
    )
    ffn_pack = lax.all_gather(ffn_pack, "wide", axis=0, tiled=True)
    columns = normed
    joined = jnp.dot(
        columns,
        attn_pack[:, :qkv_cols],
        preferred_element_type=jnp.float32,
    )
    heads_here = qkv_local.shape[1] // width
    balance = (
        jnp.exp(jnp.sum(lambdas[0] * lambdas[1], -1))
        - jnp.exp(jnp.sum(lambdas[2] * lambdas[3], -1))
        + lambda_base
    )
    outputs = []
    for prompt in range(prompts_here):
        block = joined[prompt * slots : (prompt + 1) * slots].reshape(slots, heads_here, width)
        quads = rotate(
            block[..., : 4 * HALF].reshape(slots, heads_here, 4, HALF), positions[prompt]
        ).astype(jnp.bfloat16)
        values = block[..., 4 * HALF :].astype(jnp.bfloat16)
        length = lengths[prompt]
        first_k = quads[:, :, 2]
        second_k = quads[:, :, 3]
        attended = diff_attend(
            quads[:, :, 0],
            quads[:, :, 1],
            first_k,
            second_k,
            values,
            jnp.arange(slots, dtype=jnp.int32),
            length,
            balance,
            sub_gain,
        )
        outputs.append(attended)
    attn = jnp.concatenate(outputs, axis=0)
    mix_terms = lax.dot_general(
        attn,
        attn_pack[:, qkv_cols:],
        (((1,), (1,)), ((), ())),
        preferred_element_type=jnp.float32,
    )
    mix = scatter_sum(mix_terms, "head", n_head)
    middle = (tokens.astype(jnp.float32) + mix).astype(jnp.bfloat16)
    middle_cols = gather_blocks(middle.T, "head", n_head, 0)
    flat = middle_cols.astype(jnp.float32)
    scale = lax.rsqrt(jnp.mean(flat * flat, axis=0, keepdims=True) + 1e-05)
    normed2 = (flat * scale * ffn_gain[:, None]).astype(jnp.bfloat16)
    gu_cols = gu_shape[1] * gu_shape[2]
    gate_up_full = ffn_pack[:, :gu_cols].reshape(-1, gu_shape[1], gu_shape[2])
    down_cols = ffn_pack[:, gu_cols:]
    rows_here = middle.shape[0]
    piece = rows_here // 2
    results = []
    for part in range(2):
        columns = normed2[:, part * piece : (part + 1) * piece]
        both = jnp.einsum(
            "dt,dgf->tgf",
            columns,
            gate_up_full,
            preferred_element_type=jnp.float32,
        )
        hidden = (jax.nn.silu(both[:, 0]) * both[:, 1]).astype(jnp.bfloat16)
        ffn_terms = lax.dot_general(
            hidden,
            down_cols,
            (((1,), (1,)), ((), ())),
            preferred_element_type=jnp.float32,
        )
        ffn = scatter_sum(ffn_terms, "head", n_head)
        stream = middle[part * piece : (part + 1) * piece].astype(jnp.float32)
        results.append((stream + ffn).astype(jnp.bfloat16))
    return jnp.concatenate(results, axis=0)

def solution(mesh):
    placed = (
        P("wide", "head"),
        P("wide"),
        P("wide", None),
        P(),
        P("wide", "head"),
        P(None, "head", None),
        P("head", None),
        P("head", "wide"),
        P(),
        P("wide", None, "head"),
        P("head", "wide"),
    )
    return jax.shard_map(
        body, mesh=mesh, in_specs=placed, out_specs=P("wide", "head"), check_vma=False
    )
```

```python
import jax
import jax.numpy as jnp
from jax import lax
from jax.sharding import PartitionSpec as P

HALF = 128
VDIM = 256


lambda_base = 0.2


def rms_scale(values, gain):
    flat = values.astype(jnp.float32)
    return flat * lax.rsqrt(jnp.mean(flat * flat, axis=-1, keepdims=True) + 1e-05) * gain


def rotate(quads, places):
    width = quads.shape[-1]
    half = width // 2
    freq = 10000.0 ** (-(jnp.arange(half, dtype=jnp.float32) * 2.0 / width))
    angle = places.astype(jnp.float32)[:, None] * freq[None, :]
    cosine = jnp.cos(angle)[:, None, None, :]
    sine = jnp.sin(angle)[:, None, None, :]
    first = quads[..., :half]
    second = quads[..., half:]
    return jnp.concatenate(
        [first * cosine - second * sine, second * cosine + first * sine], axis=-1
    )


def gather_blocks(x, axis, n, dim):
    spread = jnp.broadcast_to(x[None], (n,) + x.shape)
    got = lax.all_to_all(spread, axis, 0, 0, tiled=True)
    got = jnp.moveaxis(got, 0, dim)
    shape = list(x.shape)
    shape[dim] *= n
    return got.reshape(shape)


def scatter_sum(terms, axis, n):
    rows, cols = terms.shape
    parts = terms.astype(jnp.bfloat16).reshape(rows, n, cols // n)
    got = lax.all_to_all(parts, axis, 1, 1, tiled=True)
    return jnp.sum(got.astype(jnp.float32), axis=1)


def diff_attend(first_q, second_q, first_k, second_k, values, rows_at, length, balance, gain):
    scale = first_q.shape[-1] ** (-0.5)
    keys_at = jnp.arange(first_k.shape[0], dtype=jnp.int32)
    allowed = (keys_at[None, :] <= rows_at[:, None]) & (keys_at[None, :] < length)
    one = jnp.einsum("rhd,shd->hrs", first_q, first_k, preferred_element_type=jnp.float32) * scale
    two = jnp.einsum("rhd,shd->hrs", second_q, second_k, preferred_element_type=jnp.float32) * scale
    one = jax.nn.softmax(jnp.where(allowed[None], one, -1e30), axis=-1)
    two = jax.nn.softmax(jnp.where(allowed[None], two, -1e30), axis=-1)
    weights = (one - balance[:, None, None] * two).astype(jnp.bfloat16)
    merged = jnp.einsum("hrs,shv->rhv", weights, values, preferred_element_type=jnp.float32)
    merged = rms_scale(merged, gain[None]) * (1.0 - lambda_base)
    merged = jnp.where((rows_at < length)[:, None, None], merged, 0.0)
    return merged.reshape(merged.shape[0], -1).astype(jnp.bfloat16)


def body(
    tokens,
    lengths,
    positions,
    attn_gain,
    qkv_weight,
    lambdas,
    sub_gain,
    out_weight,
    ffn_gain,
    gate_up_weight,
    down_weight,
):
    prompts_here = lengths.shape[0]
    slots = positions.shape[1]
    width = 4 * HALF + VDIM
    n_head = lax.axis_size("head")
    n_wide = lax.axis_size("wide")
    full_rows = gather_blocks(tokens, "head", n_head, 1)
    normed = rms_scale(full_rows, attn_gain).astype(jnp.bfloat16)
    qkv_local = qkv_weight.astype(jnp.bfloat16)
    qkv_cols = qkv_local.shape[1]
    attn_pack = jnp.concatenate([qkv_local, out_weight.astype(jnp.bfloat16).T], axis=1)
    attn_pack = lax.all_gather(attn_pack, "wide", axis=0, tiled=True)
    gate_up_local = gate_up_weight.astype(jnp.bfloat16)
    gu_shape = gate_up_local.shape
    ffn_pack = jnp.concatenate(
        [gate_up_local.reshape(gu_shape[0], -1), down_weight.astype(jnp.bfloat16).T], axis=1
    )
    ffn_pack = lax.all_gather(ffn_pack, "wide", axis=0, tiled=True)
    columns = normed
    joined = jnp.dot(
        columns,
        attn_pack[:, :qkv_cols],
        preferred_element_type=jnp.float32,
    )
    heads_here = qkv_local.shape[1] // width
    balance = (
        jnp.exp(jnp.sum(lambdas[0] * lambdas[1], -1))
        - jnp.exp(jnp.sum(lambdas[2] * lambdas[3], -1))
        + lambda_base
    )
    outputs = []
    for prompt in range(prompts_here):
        block = joined[prompt * slots : (prompt + 1) * slots].reshape(slots, heads_here, width)
        quads = rotate(
            block[..., : 4 * HALF].reshape(slots, heads_here, 4, HALF), positions[prompt]
        ).astype(jnp.bfloat16)
        values = block[..., 4 * HALF :].astype(jnp.bfloat16)
        length = lengths[prompt]
        first_k = quads[:, :, 2]
        second_k = quads[:, :, 3]
        attended = diff_attend(
            quads[:, :, 0],
            quads[:, :, 1],
            first_k,
            second_k,
            values,
            jnp.arange(slots, dtype=jnp.int32),
            length,
            balance,
            sub_gain,
        )
        outputs.append(attended)
    attn = jnp.concatenate(outputs, axis=0)
    mix_terms = lax.dot_general(
        attn,
        attn_pack[:, qkv_cols:],
        (((1,), (1,)), ((), ())),
        preferred_element_type=jnp.float32,
    )
    mix = scatter_sum(mix_terms, "head", n_head)
    middle = (tokens.astype(jnp.float32) + mix).astype(jnp.bfloat16)
    middle_cols = gather_blocks(middle.T, "head", n_head, 0)
    flat = middle_cols.astype(jnp.float32)
    scale = lax.rsqrt(jnp.mean(flat * flat, axis=0, keepdims=True) + 1e-05)
    normed2 = (flat * scale * ffn_gain[:, None]).astype(jnp.bfloat16)
    gu_cols = gu_shape[1] * gu_shape[2]
    units = gu_shape[2]
    down_cols = ffn_pack[:, gu_cols:]
    rows_here = middle.shape[0]
    piece = rows_here // 2
    results = []
    for part in range(2):
        columns = normed2[:, part * piece : (part + 1) * piece]
        both = lax.dot_general(
            columns,
            ffn_pack[:, :gu_cols],
            (((0,), (0,)), ((), ())),
            preferred_element_type=jnp.float32,
        )
        hidden = (jax.nn.silu(both[:, :units]) * both[:, units:]).astype(jnp.bfloat16)
        ffn_terms = lax.dot_general(
            hidden,
            down_cols,
            (((1,), (1,)), ((), ())),
            preferred_element_type=jnp.float32,
        )
        ffn = scatter_sum(ffn_terms, "head", n_head)
        stream = middle[part * piece : (part + 1) * piece].astype(jnp.float32)
        results.append((stream + ffn).astype(jnp.bfloat16))
    return jnp.concatenate(results, axis=0)

def solution(mesh):
    placed = (
        P("wide", "head"),
        P("wide"),
        P("wide", None),
        P(),
        P("wide", "head"),
        P(None, "head", None),
        P("head", None),
        P("head", "wide"),
        P(),
        P("wide", None, "head"),
        P("head", "wide"),
    )
    return jax.shard_map(
        body, mesh=mesh, in_specs=placed, out_specs=P("wide", "head"), check_vma=False
    )
```

```python
import jax
import jax.numpy as jnp
from jax import lax
from jax.sharding import PartitionSpec as P

HALF = 128
VDIM = 256


lambda_base = 0.2


def rms_scale(values, gain):
    flat = values.astype(jnp.float32)
    return flat * lax.rsqrt(jnp.mean(flat * flat, axis=-1, keepdims=True) + 1e-05) * gain


def rotate(quads, places):
    width = quads.shape[-1]
    half = width // 2
    freq = 10000.0 ** (-(jnp.arange(half, dtype=jnp.float32) * 2.0 / width))
    angle = places.astype(jnp.float32)[:, None] * freq[None, :]
    cosine = jnp.cos(angle)[:, None, None, :]
    sine = jnp.sin(angle)[:, None, None, :]
    first = quads[..., :half]
    second = quads[..., half:]
    return jnp.concatenate(
        [first * cosine - second * sine, second * cosine + first * sine], axis=-1
    )


def gather_blocks(x, axis, n, dim):
    spread = jnp.broadcast_to(x[None], (n,) + x.shape)
    got = lax.all_to_all(spread, axis, 0, 0, tiled=True)
    got = jnp.moveaxis(got, 0, dim)
    shape = list(x.shape)
    shape[dim] *= n
    return got.reshape(shape)


def scatter_sum(terms, axis, n):
    rows, cols = terms.shape
    parts = terms.astype(jnp.bfloat16).reshape(rows, n, cols // n)
    got = lax.all_to_all(parts, axis, 1, 1, tiled=True)
    return jnp.sum(got.astype(jnp.float32), axis=1)


def diff_attend(first_q, second_q, first_k, second_k, values, rows_at, length, balance, gain):
    scale = first_q.shape[-1] ** (-0.5)
    keys_at = jnp.arange(first_k.shape[0], dtype=jnp.int32)
    allowed = (keys_at[None, :] <= rows_at[:, None]) & (keys_at[None, :] < length)
    one = jnp.einsum("rhd,shd->hrs", first_q, first_k, preferred_element_type=jnp.float32) * scale
    two = jnp.einsum("rhd,shd->hrs", second_q, second_k, preferred_element_type=jnp.float32) * scale
    one = jax.nn.softmax(jnp.where(allowed[None], one, -1e30), axis=-1)
    two = jax.nn.softmax(jnp.where(allowed[None], two, -1e30), axis=-1)
    weights = (one - balance[:, None, None] * two).astype(jnp.bfloat16)
    merged = jnp.einsum("hrs,shv->rhv", weights, values, preferred_element_type=jnp.float32)
    merged = rms_scale(merged, gain[None]) * (1.0 - lambda_base)
    merged = jnp.where((rows_at < length)[:, None, None], merged, 0.0)
    return merged.reshape(merged.shape[0], -1).astype(jnp.bfloat16)


def body(
    tokens,
    lengths,
    positions,
    attn_gain,
    qkv_weight,
    lambdas,
    sub_gain,
    out_weight,
    ffn_gain,
    gate_up_weight,
    down_weight,
):
    prompts_here = lengths.shape[0]
    slots = positions.shape[1]
    width = 4 * HALF + VDIM
    n_head = lax.axis_size("head")
    n_wide = lax.axis_size("wide")
    full_rows = gather_blocks(tokens, "head", n_head, 1)
    normed = rms_scale(full_rows, attn_gain).astype(jnp.bfloat16)
    qkv_local = qkv_weight.astype(jnp.bfloat16)
    qkv_cols = qkv_local.shape[1]
    attn_pack = jnp.concatenate([qkv_local, out_weight.astype(jnp.bfloat16).T], axis=1)
    attn_pack = lax.all_gather(attn_pack, "wide", axis=0, tiled=True)
    gate_up_local = gate_up_weight.astype(jnp.bfloat16)
    gu_shape = gate_up_local.shape
    ffn_pack = jnp.concatenate(
        [gate_up_local.reshape(gu_shape[0], -1), down_weight.astype(jnp.bfloat16).T], axis=1
    )
    ffn_pack = lax.all_gather(ffn_pack, "wide", axis=0, tiled=True)
    columns = normed
    joined = jnp.dot(
        columns,
        attn_pack[:, :qkv_cols],
        preferred_element_type=jnp.float32,
    )
    heads_here = qkv_local.shape[1] // width
    balance = (
        jnp.exp(jnp.sum(lambdas[0] * lambdas[1], -1))
        - jnp.exp(jnp.sum(lambdas[2] * lambdas[3], -1))
        + lambda_base
    )
    outputs = []
    for prompt in range(prompts_here):
        block = joined[prompt * slots : (prompt + 1) * slots].reshape(slots, heads_here, width)
        quads = rotate(
            block[..., : 4 * HALF].reshape(slots, heads_here, 4, HALF), positions[prompt]
        ).astype(jnp.bfloat16)
        values = block[..., 4 * HALF :].astype(jnp.bfloat16)
        length = lengths[prompt]
        first_k = quads[:, :, 2]
        second_k = quads[:, :, 3]
        attended = diff_attend(
            quads[:, :, 0],
            quads[:, :, 1],
            first_k,
            second_k,
            values,
            jnp.arange(slots, dtype=jnp.int32),
            length,
            balance,
            sub_gain,
        )
        mix_terms = lax.dot_general(
            attended,
            attn_pack[:, qkv_cols:],
            (((1,), (1,)), ((), ())),
            preferred_element_type=jnp.float32,
        )
        outputs.append(scatter_sum(mix_terms, "head", n_head))
    mix = jnp.concatenate(outputs, axis=0)
    middle = (tokens.astype(jnp.float32) + mix).astype(jnp.bfloat16)
    middle_cols = gather_blocks(middle.T, "head", n_head, 0)
    flat = middle_cols.astype(jnp.float32)
    scale = lax.rsqrt(jnp.mean(flat * flat, axis=0, keepdims=True) + 1e-05)
    normed2 = (flat * scale * ffn_gain[:, None]).astype(jnp.bfloat16)
    gu_cols = gu_shape[1] * gu_shape[2]
    units = gu_shape[2]
    down_cols = ffn_pack[:, gu_cols:]
    rows_here = middle.shape[0]
    piece = rows_here // 2
    results = []
    for part in range(2):
        columns = normed2[:, part * piece : (part + 1) * piece]
        both = lax.dot_general(
            columns,
            ffn_pack[:, :gu_cols],
            (((0,), (0,)), ((), ())),
            preferred_element_type=jnp.float32,
        )
        hidden = (jax.nn.silu(both[:, :units]) * both[:, units:]).astype(jnp.bfloat16)
        ffn_terms = lax.dot_general(
            hidden,
            down_cols,
            (((1,), (1,)), ((), ())),
            preferred_element_type=jnp.float32,
        )
        ffn = scatter_sum(ffn_terms, "head", n_head)
        stream = middle[part * piece : (part + 1) * piece].astype(jnp.float32)
        results.append((stream + ffn).astype(jnp.bfloat16))
    return jnp.concatenate(results, axis=0)

def solution(mesh):
    placed = (
        P("wide", "head"),
        P("wide"),
        P("wide", None),
        P(),
        P("wide", "head"),
        P(None, "head", None),
        P("head", None),
        P("head", "wide"),
        P(),
        P("wide", None, "head"),
        P("head", "wide"),
    )
    return jax.shard_map(
        body, mesh=mesh, in_specs=placed, out_specs=P("wide", "head"), check_vma=False
    )
```

```python
import jax
import jax.numpy as jnp
from jax import lax
from jax.sharding import PartitionSpec as P

HALF = 128
VDIM = 256


lambda_base = 0.2


def rms_scale(values, gain):
    flat = values.astype(jnp.float32)
    return flat * lax.rsqrt(jnp.mean(flat * flat, axis=-1, keepdims=True) + 1e-05) * gain


def rotate(quads, places):
    width = quads.shape[-1]
    half = width // 2
    freq = 10000.0 ** (-(jnp.arange(half, dtype=jnp.float32) * 2.0 / width))
    angle = places.astype(jnp.float32)[:, None] * freq[None, :]
    cosine = jnp.cos(angle)[:, None, None, :]
    sine = jnp.sin(angle)[:, None, None, :]
    first = quads[..., :half]
    second = quads[..., half:]
    return jnp.concatenate(
        [first * cosine - second * sine, second * cosine + first * sine], axis=-1
    )


def gather_blocks(x, axis, n, dim):
    spread = jnp.broadcast_to(x[None], (n,) + x.shape)
    got = lax.all_to_all(spread, axis, 0, 0, tiled=True)
    got = jnp.moveaxis(got, 0, dim)
    shape = list(x.shape)
    shape[dim] *= n
    return got.reshape(shape)


def scatter_sum(terms, axis, n):
    rows, cols = terms.shape
    parts = terms.astype(jnp.bfloat16).reshape(rows, n, cols // n)
    got = lax.all_to_all(parts, axis, 1, 1, tiled=True)
    return jnp.sum(got.astype(jnp.float32), axis=1)


def diff_attend(first_q, second_q, first_k, second_k, values, rows_at, length, balance, gain):
    scale = first_q.shape[-1] ** (-0.5)
    keys_at = jnp.arange(first_k.shape[0], dtype=jnp.int32)
    allowed = (keys_at[None, :] <= rows_at[:, None]) & (keys_at[None, :] < length)
    one = jnp.einsum("rhd,shd->hrs", first_q, first_k, preferred_element_type=jnp.float32) * scale
    two = jnp.einsum("rhd,shd->hrs", second_q, second_k, preferred_element_type=jnp.float32) * scale
    one = jax.nn.softmax(jnp.where(allowed[None], one, -1e30), axis=-1)
    two = jax.nn.softmax(jnp.where(allowed[None], two, -1e30), axis=-1)
    weights = (one - balance[:, None, None] * two).astype(jnp.bfloat16)
    merged = jnp.einsum("hrs,shv->rhv", weights, values, preferred_element_type=jnp.float32)
    merged = rms_scale(merged, gain[None]) * (1.0 - lambda_base)
    merged = jnp.where((rows_at < length)[:, None, None], merged, 0.0)
    return merged.reshape(merged.shape[0], -1).astype(jnp.bfloat16)


def body(
    tokens,
    lengths,
    positions,
    attn_gain,
    qkv_weight,
    lambdas,
    sub_gain,
    out_weight,
    ffn_gain,
    gate_up_weight,
    down_weight,
):
    prompts_here = lengths.shape[0]
    slots = positions.shape[1]
    width = 4 * HALF + VDIM
    n_head = lax.axis_size("head")
    n_wide = lax.axis_size("wide")
    full_rows = gather_blocks(tokens, "head", n_head, 1)
    flat_rows = full_rows.astype(jnp.float32)
    grouped = flat_rows.reshape(flat_rows.shape[0], n_head, -1)
    partial = lax.optimization_barrier(jnp.sum(grouped * grouped, axis=2))
    power = jnp.sum(partial, axis=1, keepdims=True) / flat_rows.shape[1]
    normed = (flat_rows * lax.rsqrt(power + 1e-05) * attn_gain).astype(jnp.bfloat16)
    qkv_local = qkv_weight.astype(jnp.bfloat16)
    qkv_cols = qkv_local.shape[1]
    attn_pack = jnp.concatenate([qkv_local, out_weight.astype(jnp.bfloat16).T], axis=1)
    attn_pack = lax.all_gather(attn_pack, "wide", axis=0, tiled=True)
    gate_up_local = gate_up_weight.astype(jnp.bfloat16)
    gu_shape = gate_up_local.shape
    ffn_pack = jnp.concatenate(
        [gate_up_local.reshape(gu_shape[0], -1), down_weight.astype(jnp.bfloat16).T], axis=1
    )
    ffn_pack = lax.all_gather(ffn_pack, "wide", axis=0, tiled=True)
    columns = normed
    joined = jnp.dot(
        columns,
        attn_pack[:, :qkv_cols],
        preferred_element_type=jnp.float32,
    )
    heads_here = qkv_local.shape[1] // width
    balance = (
        jnp.exp(jnp.sum(lambdas[0] * lambdas[1], -1))
        - jnp.exp(jnp.sum(lambdas[2] * lambdas[3], -1))
        + lambda_base
    )
    outputs = []
    for prompt in range(prompts_here):
        block = joined[prompt * slots : (prompt + 1) * slots].reshape(slots, heads_here, width)
        quads = rotate(
            block[..., : 4 * HALF].reshape(slots, heads_here, 4, HALF), positions[prompt]
        ).astype(jnp.bfloat16)
        values = block[..., 4 * HALF :].astype(jnp.bfloat16)
        length = lengths[prompt]
        first_k = quads[:, :, 2]
        second_k = quads[:, :, 3]
        attended = diff_attend(
            quads[:, :, 0],
            quads[:, :, 1],
            first_k,
            second_k,
            values,
            jnp.arange(slots, dtype=jnp.int32),
            length,
            balance,
            sub_gain,
        )
        outputs.append(attended)
    attn = jnp.concatenate(outputs, axis=0)
    mix_terms = lax.dot_general(
        attn,
        attn_pack[:, qkv_cols:],
        (((1,), (1,)), ((), ())),
        preferred_element_type=jnp.float32,
    )
    mix = scatter_sum(mix_terms, "head", n_head)
    middle = (tokens.astype(jnp.float32) + mix).astype(jnp.bfloat16)
    middle_cols = gather_blocks(middle.T, "head", n_head, 0)
    flat = middle_cols.astype(jnp.float32)
    grouped = flat.reshape(n_head, -1, flat.shape[1])
    partial = lax.optimization_barrier(jnp.sum(grouped * grouped, axis=1))
    power = jnp.sum(partial, axis=0, keepdims=True) / flat.shape[0]
    scale = lax.rsqrt(power + 1e-05)
    normed2 = (flat * scale * ffn_gain[:, None]).astype(jnp.bfloat16)
    gu_cols = gu_shape[1] * gu_shape[2]
    units = gu_shape[2]
    down_cols = ffn_pack[:, gu_cols:]
    rows_here = middle.shape[0]
    piece = rows_here // 2
    results = []
    for part in range(2):
        columns = normed2[:, part * piece : (part + 1) * piece]
        both = lax.dot_general(
            columns,
            ffn_pack[:, :gu_cols],
            (((0,), (0,)), ((), ())),
            preferred_element_type=jnp.float32,
        )
        hidden = (jax.nn.silu(both[:, :units]) * both[:, units:]).astype(jnp.bfloat16)
        ffn_terms = lax.dot_general(
            hidden,
            down_cols,
            (((1,), (1,)), ((), ())),
            preferred_element_type=jnp.float32,
        )
        ffn = scatter_sum(ffn_terms, "head", n_head)
        stream = middle[part * piece : (part + 1) * piece].astype(jnp.float32)
        results.append((stream + ffn).astype(jnp.bfloat16))
    return jnp.concatenate(results, axis=0)

def solution(mesh):
    placed = (
        P("wide", "head"),
        P("wide"),
        P("wide", None),
        P(),
        P("wide", "head"),
        P(None, "head", None),
        P("head", None),
        P("head", "wide"),
        P(),
        P("wide", None, "head"),
        P("head", "wide"),
    )
    return jax.shard_map(
        body, mesh=mesh, in_specs=placed, out_specs=P("wide", "head"), check_vma=False
    )
```

```python
import jax
import jax.numpy as jnp
from jax import lax
from jax.sharding import PartitionSpec as P

HALF = 128
VDIM = 256


lambda_base = 0.2


def rms_scale(values, gain):
    flat = values.astype(jnp.float32)
    return flat * lax.rsqrt(jnp.mean(flat * flat, axis=-1, keepdims=True) + 1e-05) * gain


def rotate(quads, places):
    width = quads.shape[-1]
    half = width // 2
    freq = 10000.0 ** (-(jnp.arange(half, dtype=jnp.float32) * 2.0 / width))
    angle = places.astype(jnp.float32)[:, None] * freq[None, :]
    cosine = jnp.cos(angle)[:, None, None, :]
    sine = jnp.sin(angle)[:, None, None, :]
    first = quads[..., :half]
    second = quads[..., half:]
    return jnp.concatenate(
        [first * cosine - second * sine, second * cosine + first * sine], axis=-1
    )


def gather_blocks(x, axis, n, dim):
    spread = jnp.broadcast_to(x[None], (n,) + x.shape)
    got = lax.all_to_all(spread, axis, 0, 0, tiled=True)
    got = jnp.moveaxis(got, 0, dim)
    shape = list(x.shape)
    shape[dim] *= n
    return got.reshape(shape)


def scatter_sum(terms, axis, n):
    rows, cols = terms.shape
    parts = terms.astype(jnp.bfloat16).reshape(rows, n, cols // n)
    got = lax.all_to_all(parts, axis, 1, 1, tiled=True)
    return jnp.sum(got.astype(jnp.float32), axis=1)


def diff_attend(first_q, second_q, first_k, second_k, values, rows_at, length, balance, gain):
    scale = first_q.shape[-1] ** (-0.5)
    keys_at = jnp.arange(first_k.shape[0], dtype=jnp.int32)
    allowed = (keys_at[None, :] <= rows_at[:, None]) & (keys_at[None, :] < length)
    one = jnp.einsum("rhd,shd->hrs", first_q, first_k, preferred_element_type=jnp.float32) * scale
    two = jnp.einsum("rhd,shd->hrs", second_q, second_k, preferred_element_type=jnp.float32) * scale
    one = jax.nn.softmax(jnp.where(allowed[None], one, -1e30), axis=-1)
    two = jax.nn.softmax(jnp.where(allowed[None], two, -1e30), axis=-1)
    weights = (one - balance[:, None, None] * two).astype(jnp.bfloat16)
    merged = jnp.einsum("hrs,shv->rhv", weights, values, preferred_element_type=jnp.float32)
    merged = rms_scale(merged, gain[None]) * (1.0 - lambda_base)
    merged = jnp.where((rows_at < length)[:, None, None], merged, 0.0)
    return merged.reshape(merged.shape[0], -1).astype(jnp.bfloat16)


def body(
    tokens,
    lengths,
    positions,
    attn_gain,
    qkv_weight,
    lambdas,
    sub_gain,
    out_weight,
    ffn_gain,
    gate_up_weight,
    down_weight,
):
    prompts_here = lengths.shape[0]
    slots = positions.shape[1]
    width = 4 * HALF + VDIM
    n_head = lax.axis_size("head")
    n_wide = lax.axis_size("wide")
    full_rows = gather_blocks(tokens, "head", n_head, 1)
    normed = rms_scale(full_rows, attn_gain).astype(jnp.bfloat16)
    qkv_local = qkv_weight.astype(jnp.bfloat16)
    qkv_cols = qkv_local.shape[1]
    attn_pack = jnp.concatenate([qkv_local, out_weight.astype(jnp.bfloat16).T], axis=1)
    attn_pack = lax.all_gather(attn_pack, "wide", axis=0, tiled=True)
    gate_up_local = gate_up_weight.astype(jnp.bfloat16)
    gu_shape = gate_up_local.shape
    ffn_pack = jnp.concatenate(
        [gate_up_local.reshape(gu_shape[0], -1), down_weight.astype(jnp.bfloat16).T], axis=1
    )
    ffn_pack = lax.all_gather(ffn_pack, "wide", axis=0, tiled=True)
    columns = normed
    joined = jnp.dot(
        columns,
        attn_pack[:, :qkv_cols],
        preferred_element_type=jnp.float32,
    )
    heads_here = qkv_local.shape[1] // width
    balance = (
        jnp.exp(jnp.sum(lambdas[0] * lambdas[1], -1))
        - jnp.exp(jnp.sum(lambdas[2] * lambdas[3], -1))
        + lambda_base
    )
    outputs = []
    for prompt in range(prompts_here):
        block = joined[prompt * slots : (prompt + 1) * slots].reshape(slots, heads_here, width)
        quads = rotate(
            block[..., : 4 * HALF].reshape(slots, heads_here, 4, HALF), positions[prompt]
        ).astype(jnp.bfloat16)
        values = block[..., 4 * HALF :].astype(jnp.bfloat16)
        length = lengths[prompt]
        first_k = quads[:, :, 2]
        second_k = quads[:, :, 3]
        attended = diff_attend(
            quads[:, :, 0],
            quads[:, :, 1],
            first_k,
            second_k,
            values,
            jnp.arange(slots, dtype=jnp.int32),
            length,
            balance,
            sub_gain,
        )
        outputs.append(attended)
    attn = jnp.concatenate(outputs, axis=0)
    mix_terms = lax.dot_general(
        attn,
        attn_pack[:, qkv_cols:],
        (((1,), (1,)), ((), ())),
        preferred_element_type=jnp.float32,
    )
    mix = scatter_sum(mix_terms, "head", n_head)
    middle = (tokens.astype(jnp.float32) + mix).astype(jnp.bfloat16)
    middle_cols = gather_blocks(middle.T, "head", n_head, 0)
    flat = middle_cols.astype(jnp.float32)
    scale = lax.rsqrt(jnp.mean(flat * flat, axis=0, keepdims=True) + 1e-05)
    normed2 = (flat * scale * ffn_gain[:, None]).astype(jnp.bfloat16)
    gu_cols = gu_shape[1] * gu_shape[2]
    units = gu_shape[2]
    down_cols = ffn_pack[:, gu_cols:]
    rows_here = middle.shape[0]
    cuts = (0, rows_here * 3 // 8, rows_here)
    results = []
    for part in range(2):
        columns = normed2[:, cuts[part] : cuts[part + 1]]
        both = lax.dot_general(
            columns,
            ffn_pack[:, :gu_cols],
            (((0,), (0,)), ((), ())),
            preferred_element_type=jnp.float32,
        )
        hidden = (jax.nn.silu(both[:, :units]) * both[:, units:]).astype(jnp.bfloat16)
        ffn_terms = lax.dot_general(
            hidden,
            down_cols,
            (((1,), (1,)), ((), ())),
            preferred_element_type=jnp.float32,
        )
        ffn = scatter_sum(ffn_terms, "head", n_head)
        stream = middle[cuts[part] : cuts[part + 1]].astype(jnp.float32)
        results.append((stream + ffn).astype(jnp.bfloat16))
    return jnp.concatenate(results, axis=0)

def solution(mesh):
    placed = (
        P("wide", "head"),
        P("wide"),
        P("wide", None),
        P(),
        P("wide", "head"),
        P(None, "head", None),
        P("head", None),
        P("head", "wide"),
        P(),
        P("wide", None, "head"),
        P("head", "wide"),
    )
    return jax.shard_map(
        body, mesh=mesh, in_specs=placed, out_specs=P("wide", "head"), check_vma=False
    )
```

```python
import jax
import jax.numpy as jnp
from jax import lax
from jax.sharding import PartitionSpec as P

HALF = 128
VDIM = 256


lambda_base = 0.2


def rms_scale(values, gain):
    flat = values.astype(jnp.float32)
    return flat * lax.rsqrt(jnp.mean(flat * flat, axis=-1, keepdims=True) + 1e-05) * gain


def rotate(quads, places):
    width = quads.shape[-1]
    half = width // 2
    freq = 10000.0 ** (-(jnp.arange(half, dtype=jnp.float32) * 2.0 / width))
    angle = places.astype(jnp.float32)[:, None] * freq[None, :]
    cosine = jnp.cos(angle)[:, None, None, :]
    sine = jnp.sin(angle)[:, None, None, :]
    first = quads[..., :half]
    second = quads[..., half:]
    return jnp.concatenate(
        [first * cosine - second * sine, second * cosine + first * sine], axis=-1
    )


def gather_blocks(x, axis, n, dim):
    spread = jnp.broadcast_to(x[None], (n,) + x.shape)
    got = lax.all_to_all(spread, axis, 0, 0, tiled=True)
    got = jnp.moveaxis(got, 0, dim)
    shape = list(x.shape)
    shape[dim] *= n
    return got.reshape(shape)


def scatter_sum(terms, axis, n):
    rows, cols = terms.shape
    parts = terms.astype(jnp.bfloat16).reshape(rows, n, cols // n)
    got = lax.all_to_all(parts, axis, 1, 1, tiled=True)
    return jnp.sum(got.astype(jnp.float32), axis=1)


def diff_attend(first_q, second_q, first_k, second_k, values, rows_at, length, balance, gain):
    scale = first_q.shape[-1] ** (-0.5)
    keys_at = jnp.arange(first_k.shape[0], dtype=jnp.int32)
    allowed = (keys_at[None, :] <= rows_at[:, None]) & (keys_at[None, :] < length)
    one = jnp.einsum("rhd,shd->hrs", first_q, first_k, preferred_element_type=jnp.float32) * scale
    two = jnp.einsum("rhd,shd->hrs", second_q, second_k, preferred_element_type=jnp.float32) * scale
    one = jax.nn.softmax(jnp.where(allowed[None], one, -1e30), axis=-1)
    two = jax.nn.softmax(jnp.where(allowed[None], two, -1e30), axis=-1)
    weights = (one - balance[:, None, None] * two).astype(jnp.bfloat16)
    merged = jnp.einsum("hrs,shv->rhv", weights, values, preferred_element_type=jnp.float32)
    merged = rms_scale(merged, gain[None]) * (1.0 - lambda_base)
    merged = jnp.where((rows_at < length)[:, None, None], merged, 0.0)
    return merged.reshape(merged.shape[0], -1).astype(jnp.bfloat16)


def body(
    tokens,
    lengths,
    positions,
    attn_gain,
    qkv_weight,
    lambdas,
    sub_gain,
    out_weight,
    ffn_gain,
    gate_up_weight,
    down_weight,
):
    prompts_here = lengths.shape[0]
    slots = positions.shape[1]
    width = 4 * HALF + VDIM
    n_head = lax.axis_size("head")
    n_wide = lax.axis_size("wide")
    full_rows = gather_blocks(tokens, "head", n_head, 1)
    normed = rms_scale(full_rows, attn_gain).astype(jnp.bfloat16)
    qkv_local = qkv_weight.astype(jnp.bfloat16)
    qkv_cols = qkv_local.shape[1]
    attn_pack = jnp.concatenate([qkv_local, out_weight.astype(jnp.bfloat16).T], axis=1)
    attn_pack = lax.all_gather(attn_pack, "wide", axis=0, tiled=True)
    gate_up_local = gate_up_weight.astype(jnp.bfloat16)
    gu_shape = gate_up_local.shape
    ffn_pack = jnp.concatenate(
        [gate_up_local.reshape(gu_shape[0], -1), down_weight.astype(jnp.bfloat16).T], axis=1
    )
    ffn_pack = lax.all_gather(ffn_pack, "wide", axis=0, tiled=True)
    columns = normed
    joined = jnp.dot(
        columns,
        attn_pack[:, :qkv_cols],
        preferred_element_type=jnp.float32,
    )
    heads_here = qkv_local.shape[1] // width
    balance = (
        jnp.exp(jnp.sum(lambdas[0] * lambdas[1], -1))
        - jnp.exp(jnp.sum(lambdas[2] * lambdas[3], -1))
        + lambda_base
    )
    outputs = []
    for prompt in range(prompts_here):
        block = joined[prompt * slots : (prompt + 1) * slots].reshape(slots, heads_here, width)
        quads = rotate(
            block[..., : 4 * HALF].reshape(slots, heads_here, 4, HALF), positions[prompt]
        ).astype(jnp.bfloat16)
        values = block[..., 4 * HALF :].astype(jnp.bfloat16)
        length = lengths[prompt]
        first_k = quads[:, :, 2]
        second_k = quads[:, :, 3]
        attended = diff_attend(
            quads[:, :, 0],
            quads[:, :, 1],
            first_k,
            second_k,
            values,
            jnp.arange(slots, dtype=jnp.int32),
            length,
            balance,
            sub_gain,
        )
        outputs.append(attended)
    attn = jnp.concatenate(outputs, axis=0)
    mix_terms = lax.dot_general(
        attn,
        attn_pack[:, qkv_cols:],
        (((1,), (1,)), ((), ())),
        preferred_element_type=jnp.float32,
    )
    mix = scatter_sum(mix_terms, "head", n_head)
    middle = (tokens.astype(jnp.float32) + mix).astype(jnp.bfloat16)
    middle_cols = gather_blocks(middle.T, "head", n_head, 0)
    flat = middle_cols.astype(jnp.float32)
    scale = lax.rsqrt(jnp.mean(flat * flat, axis=0, keepdims=True) + 1e-05)
    normed2 = (flat * scale * ffn_gain[:, None]).astype(jnp.bfloat16)
    gu_cols = gu_shape[1] * gu_shape[2]
    units = gu_shape[2]
    down_cols = ffn_pack[:, gu_cols:]
    rows_here = middle.shape[0]
    cuts = (0, rows_here // 4, rows_here)
    results = []
    for part in range(2):
        columns = normed2[:, cuts[part] : cuts[part + 1]]
        both = lax.dot_general(
            columns,
            ffn_pack[:, :gu_cols],
            (((0,), (0,)), ((), ())),
            preferred_element_type=jnp.float32,
        )
        hidden = (jax.nn.silu(both[:, :units]) * both[:, units:]).astype(jnp.bfloat16)
        ffn_terms = lax.dot_general(
            hidden,
            down_cols,
            (((1,), (1,)), ((), ())),
            preferred_element_type=jnp.float32,
        )
        ffn = scatter_sum(ffn_terms, "head", n_head)
        stream = middle[cuts[part] : cuts[part + 1]].astype(jnp.float32)
        results.append((stream + ffn).astype(jnp.bfloat16))
    return jnp.concatenate(results, axis=0)

def solution(mesh):
    placed = (
        P("wide", "head"),
        P("wide"),
        P("wide", None),
        P(),
        P("wide", "head"),
        P(None, "head", None),
        P("head", None),
        P("head", "wide"),
        P(),
        P("wide", None, "head"),
        P("head", "wide"),
    )
    return jax.shard_map(
        body, mesh=mesh, in_specs=placed, out_specs=P("wide", "head"), check_vma=False
    )
```
